512 devices in a mesh: gx: 8 (over x, core), yz: 64 (over y, z).
Axes of the slice: x: 4, y: 8, z: 8, core: 2. Of those that a mesh axis runs over, the one named last changes fastest.
Arguments:
- old_coeff: bfloat16 [131072, 512], P(('gx', 'yz')), may hold values from -6 to 6
- basis_old: bfloat16 [8, 64, 64], replicated, may hold values from -0.75 to 0.75
- basis_new: bfloat16 [8, 64, 64], replicated, may hold values from -0.75 to 0.75
- quad_weight: float32 [8, 64], replicated, may hold values from 0.3 to 3
- tet_zone: int32 [1048576], P(('gx', 'yz')), may hold values from 0 to 255
- tet_table: int32 [1048576], P(('gx', 'yz')), may hold values from 0 to 7
- tet_volume: float32 [1048576], P(('gx', 'yz')), may hold values from 0.1 to 1
- tet_dest: int32 [1048576], P(('gx', 'yz')), may hold values from 0 to 415, as said below
- recv_list: int32 [512, 160], P(('gx', 'yz')), may hold values from 0 to 255
- inv_mass: bfloat16 [131072, 4096], P(('gx', 'yz')), may hold values from -0.75 to 0.75
Outputs:
- new_coeff: float32 [131072, 512], P(('gx', 'yz'))
The draws below stay inside these ranges and needn't reach their ends.
Inputs may be any that keep to these rules, and one draw needn't show every extreme that they name: `tet_dest`: A value below 256 names an own new zone; 256 + k * 16 + s names slot s of partner k.
All inputs are finite; a program needn't handle non-finite values.
Results may differ from the reference program's by a relative error of at most 0.0042.
Values may be sent and summed in bfloat16 or wider, within the bound.
No kernel may reach another device: no remote copies, remote signals or barrier semaphores. Data moves between devices by JAX's collectives and lax.ppermute only.
A program may use at most 64 MiB of HBM per device.

```python
import math
import jax
import jax.numpy as jnp
from jax import lax

NB = 64
NF = 8
Q = 64
NTAB = 8
PARTNERS = 10
ZONE_DEV = 256
TET_DEV = 2048
CAP = 16
FACE = 8
ZONES = 131072
TETS = 1048576
N_GX = 8
N_YZ = 64
DEVICES = 512


def draw_tet_dest(key, part):
    device_count = TETS // TET_DEV
    keys_all = jax.random.split(key, 5)
    share_draw = jax.random.randint(keys_all[0], (device_count, TET_DEV), 0, 100)
    own_zone = jax.random.randint(keys_all[1], (device_count, TET_DEV), 0, ZONE_DEV)
    far_slot = ZONE_DEV + jax.random.randint(keys_all[2], (device_count, TET_DEV), 0, PARTNERS * CAP)
    dest_value = jnp.where(share_draw < 82, own_zone, far_slot)
    first_place = jax.random.randint(keys_all[3], (device_count, 1), 0, TET_DEV)
    second_place = (first_place + 1 + jax.random.randint(keys_all[4], (device_count, 1), 0, TET_DEV - 1)) % TET_DEV
    column_ids = jnp.arange(TET_DEV, dtype=jnp.int32)[None, :]
    dest_value = jnp.where(column_ids == first_place, ZONE_DEV + PARTNERS * CAP - 1, dest_value)
    dest_value = jnp.where(column_ids == second_place, 0, dest_value)
    return dest_value.reshape(device_count * TET_DEV).astype(jnp.int32)


def place_ends(values, own_key, least, high):
    index_at = [jax.random.randint(jax.random.fold_in(own_key, axis), (), 0, length) for axis, length in enumerate(values.shape)]
    widest = values.shape.index(max(values.shape))
    neighbour = index_at[:widest] + [(index_at[widest] + 1) % values.shape[widest]] + index_at[widest + 1:]
    return values.at[tuple(index_at)].set(least).at[tuple(neighbour)].set(high)


def level_of(own_key, extent, cuts, smallest, top_value):
    gain, own = 1.0, jax.random.fold_in(own_key, 6)
    for axis_at, blocks in cuts:
        draws = jnp.exp(jax.random.uniform(jax.random.fold_in(own, axis_at), (blocks,), jnp.float32, smallest / len(cuts), top_value / len(cuts)))
        gain = gain * jnp.repeat(draws, extent[axis_at] // blocks).reshape([-1 if axis == axis_at else 1 for axis in range(len(extent))])
    return gain


def centred(stream_key, shape, width, bound, cuts=(), held_as=jnp.bfloat16):
    values = width * jax.random.normal(stream_key, shape, jnp.float32)
    if cuts:
        values = values * level_of(stream_key, shape, cuts, -0.22, 0.18)
    return jnp.clip(values, -bound, bound).astype(held_as)


def setup_inputs(seed: int = 0) -> dict:
    key_of = jax.random.split(jax.random.key(seed), 11)
    old_coeff = centred(key_of[0], (ZONES, NB * NF), 1.0, 6.0, ((0, 512),))
    basis_old = centred(key_of[1], (NTAB, Q, NB), NB ** -0.5, 0.75)
    basis_new = centred(key_of[2], (NTAB, Q, NB), Q ** -0.5, 0.75)
    quad_weight = jnp.clip(jnp.exp(jax.random.uniform(key_of[3], (NTAB, Q), jnp.float32, math.log(0.3), math.log(3.0))), 0.3, 3.0)
    tet_zone = place_ends(jax.random.randint(key_of[4], (TETS,), 0, ZONE_DEV), jax.random.fold_in(key_of[4], 1), 0, ZONE_DEV - 1).astype(jnp.int32)
    tet_table = place_ends(jax.random.randint(key_of[5], (TETS,), 0, NTAB), jax.random.fold_in(key_of[5], 1), 0, NTAB - 1).astype(jnp.int32)
    tet_volume = jnp.clip(jnp.exp(math.log(1.0) - 2.3025851 * jax.random.uniform(key_of[6], (TETS,), jnp.float32) ** level_of(key_of[6], (TETS,), ((0, 512),), -0.2, 0.2)), 0.1, 1.0)
    tet_dest = draw_tet_dest(jax.random.fold_in(key_of[10], 71), 0)
    recv_list = place_ends(jax.random.randint(key_of[8], (DEVICES, PARTNERS * CAP), 0, ZONE_DEV), jax.random.fold_in(key_of[8], 1), 0, ZONE_DEV - 1).astype(jnp.int32)
    inv_mass = centred(key_of[9], (ZONES, NB * NB), NB ** -0.5, 0.75, ((0, 512),))
    return {"old_coeff": old_coeff, "basis_old": basis_old, "basis_new": basis_new, "quad_weight": quad_weight, "tet_zone": tet_zone, "tet_table": tet_table, "tet_volume": tet_volume, "tet_dest": tet_dest, "recv_list": recv_list, "inv_mass": inv_mass}


def reference(old_coeff, basis_old, basis_new, quad_weight, tet_zone, tet_table, tet_volume, tet_dest, recv_list, inv_mass):
    row_count = ZONE_DEV + PARTNERS * CAP
    row_width = NB * NF
    coeff_dev = old_coeff.reshape(DEVICES, ZONE_DEV, NB, NF)
    zone_dev = tet_zone.reshape(DEVICES, TET_DEV)
    table_dev = tet_table.reshape(DEVICES, TET_DEV)
    volume_dev = tet_volume.reshape(DEVICES, TET_DEV)
    dest_dev = tet_dest.reshape(DEVICES, TET_DEV)

    def one_device(pieces):
        coeff_one, zone_one, table_one, volume_one, dest_one = pieces
        picked = coeff_one[zone_one].astype(jnp.float32)
        old_rows = basis_old[table_one].astype(jnp.float32)
        values = jnp.einsum("eqi,eif->eqf", old_rows, picked)
        scaling = quad_weight[table_one] * volume_one[:, None]
        weighted = (scaling[:, :, None] * values).astype(jnp.bfloat16)
        new_rows = basis_new[table_one].astype(jnp.float32)
        moment = jnp.einsum("eqj,eqf->ejf", new_rows, weighted.astype(jnp.float32))
        return jax.ops.segment_sum(moment.reshape(TET_DEV, row_width), dest_one, num_segments=row_count)

    partial_value = lax.map(one_device, (coeff_dev, zone_dev, table_dev, volume_dev, dest_dev))
    own_part = partial_value[:, :ZONE_DEV]
    sent = partial_value[:, ZONE_DEV:].astype(jnp.bfloat16).reshape(N_GX, N_YZ, PARTNERS, CAP, row_width)
    offsets = [1, -1, FACE, -FACE, FACE + 1, -FACE - 1, FACE - 1, 1 - FACE]
    arrived = []
    for partner in range(8):
        arrived.append(jnp.roll(sent[:, :, partner], offsets[partner], axis=1))
    arrived.append(jnp.roll(sent[:, :, 8], 1, axis=0))
    arrived.append(jnp.roll(sent[:, :, 9], -1, axis=0))
    received = jnp.stack(arrived, axis=2).reshape(DEVICES, PARTNERS * CAP, row_width)
    inverse_dev = inv_mass.reshape(DEVICES, ZONE_DEV, NB, NB)

    def finish(pieces):
        own_one, received_one, list_one, inverse_one = pieces
        gathered = own_one + jax.ops.segment_sum(received_one.astype(jnp.float32), list_one, num_segments=ZONE_DEV)
        rounded = gathered.astype(jnp.bfloat16).reshape(ZONE_DEV, NB, NF)
        result = jnp.einsum("zjk,zkf->zjf", inverse_one.astype(jnp.float32), rounded.astype(jnp.float32))
        return result.reshape(ZONE_DEV, row_width)

    new_coeff = lax.map(finish, (own_part, received, recv_list, inverse_dev))
    return new_coeff.reshape(DEVICES * ZONE_DEV, row_width)
```

```python
import functools

import jax
import jax.numpy as jnp
from jax import lax
from jax.experimental import pallas as pl
from jax.experimental.pallas import tpu as pltpu
from jax.sharding import PartitionSpec as P

F32 = jnp.float32
BF16 = jnp.bfloat16


def tet_kernel(
    zone_ref, table_ref, vol_ref, dest_ref, ct_ref, bold_ref, bnewt_ref, qwt_ref, out_ref, mom_ref,
    *, tables, basis, fields, zones, rows_pad
):
    step = pl.program_id(0)

    @pl.when(step == 0)
    def _():
        out_ref[...] = jnp.zeros_like(out_ref)

    block = zone_ref.shape[1]
    zone = zone_ref[...]
    zone_hot = (lax.broadcasted_iota(jnp.int32, (zones, block), 0) == zone).astype(BF16)
    picked = jnp.dot(ct_ref[...], zone_hot, preferred_element_type=F32).astype(BF16)
    table = table_ref[...]
    masks = [table == t for t in range(tables)]
    qwt = qwt_ref[...]
    scale = jnp.broadcast_to(qwt[:, 0:1], (basis, block))
    for t in range(1, tables):
        scale = jnp.where(masks[t], qwt[:, t : t + 1], scale)
    scale = scale * vol_ref[...]
    bold = bold_ref[...]
    bnewt = bnewt_ref[...]
    for f in range(fields):
        every = jnp.dot(bold, picked[f * basis : (f + 1) * basis, :], preferred_element_type=F32)
        values = every[0:basis]
        for t in range(1, tables):
            values = jnp.where(masks[t], every[t * basis : (t + 1) * basis], values)
        weighted = (scale * values).astype(BF16)
        every = jnp.dot(bnewt, weighted, preferred_element_type=F32)
        moment = every[0:basis]
        for t in range(1, tables):
            moment = jnp.where(masks[t], every[t * basis : (t + 1) * basis], moment)
        mom_ref[f * basis : (f + 1) * basis, :] = moment
    moments = mom_ref[...]
    high = moments.astype(BF16)
    low = (moments - high.astype(F32)).astype(BF16)
    dest_hot = (lax.broadcasted_iota(jnp.int32, (block, rows_pad), 1) == dest_ref[...]).astype(BF16)
    out_ref[...] += jnp.dot(high, dest_hot, preferred_element_type=F32) + jnp.dot(
        low, dest_hot, preferred_element_type=F32
    )


def tet_partials(coeff_t, bold, bnewt, qwt, zone, table, vol, dest, rows_pad, block):
    tet_count = zone.shape[0]
    width, zones = coeff_t.shape
    tables = qwt.shape[1]
    basis = bold.shape[1]
    fields = width // basis
    kernel = functools.partial(
        tet_kernel, tables=tables, basis=basis, fields=fields, zones=zones, rows_pad=rows_pad
    )
    row_spec = pl.BlockSpec((1, block), lambda i: (0, i))
    whole = lambda shape: pl.BlockSpec(shape, lambda i: (0, 0))
    return pl.pallas_call(
        kernel,
        grid=(tet_count // block,),
        in_specs=[
            row_spec,
            row_spec,
            row_spec,
            pl.BlockSpec((block, 1), lambda i: (i, 0)),
            whole(coeff_t.shape),
            whole(bold.shape),
            whole(bnewt.shape),
            whole(qwt.shape),
        ],
        out_specs=whole((width, rows_pad)),
        out_shape=jax.ShapeDtypeStruct((width, rows_pad), F32),
        scratch_shapes=[pltpu.VMEM((width, block), F32)],
        compiler_params=pltpu.CompilerParams(dimension_semantics=("arbitrary",)),
    )(
        zone.reshape(1, tet_count),
        table.reshape(1, tet_count),
        vol.reshape(1, tet_count),
        dest.reshape(tet_count, 1),
        coeff_t,
        bold,
        bnewt,
        qwt,
    )


def shifted(block, axis, distance):
    count = lax.axis_size(axis)
    route = [(i, (i + distance) % count) for i in range(count)]
    return lax.ppermute(block, axis, route)


def on_device(
    old_coeff,
    basis_old,
    basis_new,
    quad_weight,
    tet_zone,
    tet_table,
    tet_volume,
    tet_dest,
    recv_list,
    inv_mass,
):
    zone_count, row_width = old_coeff.shape
    tables, quad, basis = basis_old.shape
    fields = row_width // basis
    slot_total = recv_list.shape[1]
    partner_count = 10
    slot_cap = slot_total // partner_count
    row_count = zone_count + slot_total
    rows_pad = -(-row_count // 128) * 128
    block = min(512, tet_zone.shape[0])

    coeff_t = old_coeff.reshape(zone_count, basis, fields).transpose(2, 1, 0).reshape(row_width, zone_count)
    bold = basis_old.reshape(tables * quad, basis)
    bnewt = basis_new.transpose(0, 2, 1).reshape(tables * basis, quad)
    qwt = quad_weight.T
    partial_t = tet_partials(
        coeff_t, bold, bnewt, qwt, tet_zone, tet_table, tet_volume, tet_dest, rows_pad, block
    )
    own_t = partial_t[:, :zone_count]
    outgoing = partial_t[:, zone_count:row_count].astype(BF16)

    lane_count = lax.axis_size("yz")
    face_side = 1 << (lane_count.bit_length() - 1) // 2
    offsets = [1, -1, face_side, -face_side, face_side + 1, -face_side - 1, face_side - 1, 1 - face_side]
    arrived = []
    for k in range(partner_count):
        piece = outgoing[:, k * slot_cap : (k + 1) * slot_cap]
        if k < 8:
            arrived.append(shifted(piece, "yz", offsets[k]))
        else:
            arrived.append(shifted(piece, "gx", 1 if k == 8 else -1))
    received_t = jnp.concatenate(arrived, axis=1)
    slot_hot = (recv_list[0][:, None] == jnp.arange(zone_count, dtype=jnp.int32)[None, :]).astype(BF16)
    gathered_t = own_t + jnp.dot(received_t, slot_hot, preferred_element_type=F32)
    rounded_t = gathered_t.astype(BF16).reshape(fields, basis, zone_count)
    rounded = rounded_t.transpose(2, 1, 0)
    inverse = inv_mass.reshape(zone_count, basis, basis)
    result = jnp.einsum("zjk,zkf->zjf", inverse, rounded, preferred_element_type=F32)
    return result.reshape(zone_count, row_width)


def solution(mesh):
    placed = (
        P(("gx", "yz"), None),
        P(),
        P(),
        P(),
        P(("gx", "yz")),
        P(("gx", "yz")),
        P(("gx", "yz")),
        P(("gx", "yz")),
        P(("gx", "yz"), None),
        P(("gx", "yz"), None),
    )
    return jax.shard_map(
        on_device, mesh=mesh, in_specs=placed, out_specs=P(("gx", "yz"), None), check_vma=False
    )
```

```python
import functools

import jax
import jax.numpy as jnp
from jax import lax
from jax.experimental import pallas as pl
from jax.experimental.pallas import tpu as pltpu
from jax.sharding import PartitionSpec as P

F32 = jnp.float32
BF16 = jnp.bfloat16


def tet_kernel(
    zone_ref, table_ref, vol_ref, dest_ref, ct_ref, bold_ref, bnewt_ref, qwt_ref, own_ref, slot_ref, mom_ref,
    *, tables, basis, fields, zones, slots_pad
):
    step = pl.program_id(0)

    @pl.when(step == 0)
    def _():
        own_ref[...] = jnp.zeros_like(own_ref)
        slot_ref[...] = jnp.zeros_like(slot_ref)

    block = zone_ref.shape[1]
    zone = zone_ref[...]
    zone_hot = (lax.broadcasted_iota(jnp.int32, (zones, block), 0) == zone).astype(BF16)
    picked = jnp.dot(ct_ref[...], zone_hot, preferred_element_type=F32).astype(BF16)
    table = table_ref[...]
    masks = [table == t for t in range(tables)]
    qwt = qwt_ref[...]
    scale = jnp.broadcast_to(qwt[:, 0:1], (basis, block))
    for t in range(1, tables):
        scale = jnp.where(masks[t], qwt[:, t : t + 1], scale)
    scale = scale * vol_ref[...]
    bold = bold_ref[...]
    bnewt = bnewt_ref[...]
    for f in range(fields):
        every = jnp.dot(bold, picked[f * basis : (f + 1) * basis, :], preferred_element_type=F32)
        values = every[0:basis]
        for t in range(1, tables):
            values = jnp.where(masks[t], every[t * basis : (t + 1) * basis], values)
        weighted = (scale * values).astype(BF16)
        every = jnp.dot(bnewt, weighted, preferred_element_type=F32)
        moment = every[0:basis]
        for t in range(1, tables):
            moment = jnp.where(masks[t], every[t * basis : (t + 1) * basis], moment)
        mom_ref[f * basis : (f + 1) * basis, :] = moment
    moments = mom_ref[...]
    high = moments.astype(BF16)
    low = (moments - high.astype(F32)).astype(BF16)
    dest = dest_ref[...]
    nt = (((1,), (1,)), ((), ()))
    own_hot = (lax.broadcasted_iota(jnp.int32, (zones, block), 0) == dest).astype(BF16)
    own_ref[...] += lax.dot_general(high, own_hot, nt, preferred_element_type=F32) + lax.dot_general(
        low, own_hot, nt, preferred_element_type=F32
    )
    slot_hot = (lax.broadcasted_iota(jnp.int32, (slots_pad, block), 0) + zones == dest).astype(BF16)
    slot_ref[...] += lax.dot_general(slot_hot, high, nt, preferred_element_type=F32) + lax.dot_general(
        slot_hot, low, nt, preferred_element_type=F32
    )


def tet_partials(coeff_t, bold, bnewt, qwt, zone, table, vol, dest, slots_pad, block):
    tet_count = zone.shape[0]
    width, zones = coeff_t.shape
    tables = qwt.shape[1]
    basis = bold.shape[1]
    fields = width // basis
    kernel = functools.partial(
        tet_kernel, tables=tables, basis=basis, fields=fields, zones=zones, slots_pad=slots_pad
    )
    row_spec = pl.BlockSpec((1, block), lambda i: (0, i))
    whole = lambda shape: pl.BlockSpec(shape, lambda i: (0, 0))
    return pl.pallas_call(
        kernel,
        grid=(tet_count // block,),
        in_specs=[
            row_spec,
            row_spec,
            row_spec,
            row_spec,
            whole(coeff_t.shape),
            whole(bold.shape),
            whole(bnewt.shape),
            whole(qwt.shape),
        ],
        out_specs=[whole((width, zones)), whole((slots_pad, width))],
        out_shape=[
            jax.ShapeDtypeStruct((width, zones), F32),
            jax.ShapeDtypeStruct((slots_pad, width), F32),
        ],
        scratch_shapes=[pltpu.VMEM((width, block), F32)],
        compiler_params=pltpu.CompilerParams(dimension_semantics=("arbitrary",)),
    )(
        zone.reshape(1, tet_count),
        table.reshape(1, tet_count),
        vol.reshape(1, tet_count),
        dest.reshape(1, tet_count),
        coeff_t,
        bold,
        bnewt,
        qwt,
    )


def finish_kernel(own_ref, recv_ref, list_ref, inv_ref, out_ref, g_ref, h_ref, invt_ref, acc_ref, *, basis, fields):
    width, zones = own_ref.shape
    slots = recv_ref.shape[0]
    slot_hot = (lax.broadcasted_iota(jnp.int32, (zones, slots), 0) == list_ref[...]).astype(F32)
    arrived = jnp.dot(slot_hot, recv_ref[...].astype(F32), preferred_element_type=F32)
    rounded = (own_ref[...] + arrived.T).astype(BF16).astype(F32)
    lanes = 128
    halves = zones // lanes
    for half in range(halves):
        g_ref[half * width : (half + 1) * width, :] = rounded[:, half * lanes : (half + 1) * lanes]
    for k in range(basis):
        for half in range(halves):
            h_ref[k * fields : (k + 1) * fields, half * lanes : (half + 1) * lanes] = g_ref[
                pl.ds(half * width + k, fields, stride=basis), :
            ]
    chunk = 128
    for c in range(basis * basis // chunk):
        invt_ref[c * chunk : (c + 1) * chunk, :] = inv_ref[:, c * chunk : (c + 1) * chunk].astype(F32).T

    def body(j, carry):
        acc = jnp.zeros((fields, zones), F32)
        for k in range(basis):
            acc = acc + invt_ref[pl.ds(j * basis + k, 1), :] * h_ref[k * fields : (k + 1) * fields, :]
        acc_ref[pl.ds(pl.multiple_of(j * fields, fields), fields), :] = acc
        return carry

    lax.fori_loop(0, basis, body, 0)
    out_ref[...] = acc_ref[...].T


def finish(own_t, received, recv_row, inv_mass, basis, fields):
    width, zones = own_t.shape
    kernel = functools.partial(finish_kernel, basis=basis, fields=fields)
    return pl.pallas_call(
        kernel,
        out_shape=jax.ShapeDtypeStruct((zones, width), F32),
        scratch_shapes=[
            pltpu.VMEM((zones // 128 * width, 128), F32),
            pltpu.VMEM((width, zones), F32),
            pltpu.VMEM((basis * basis, zones), F32),
            pltpu.VMEM((width, zones), F32),
        ],
    )(own_t, received, recv_row, inv_mass)


def shifted(block, axis, distance):
    count = lax.axis_size(axis)
    route = [(i, (i + distance) % count) for i in range(count)]
    return lax.ppermute(block, axis, route)


def on_device(
    old_coeff,
    basis_old,
    basis_new,
    quad_weight,
    tet_zone,
    tet_table,
    tet_volume,
    tet_dest,
    recv_list,
    inv_mass,
):
    zone_count, row_width = old_coeff.shape
    tables, quad, basis = basis_old.shape
    fields = row_width // basis
    slot_total = recv_list.shape[1]
    partner_count = 10
    slot_cap = slot_total // partner_count
    slots_pad = -(-slot_total // 128) * 128
    block = min(512, tet_zone.shape[0])

    coeff_t = old_coeff.reshape(zone_count, basis, fields).transpose(2, 1, 0).reshape(row_width, zone_count)
    bold = basis_old.reshape(tables * quad, basis)
    bnewt = basis_new.transpose(0, 2, 1).reshape(tables * basis, quad)
    qwt = quad_weight.T
    own_t, slot_rows = tet_partials(
        coeff_t, bold, bnewt, qwt, tet_zone, tet_table, tet_volume, tet_dest, slots_pad, block
    )
    outgoing = slot_rows[:slot_total].astype(BF16).reshape(partner_count, slot_cap, row_width)

    lane_count = lax.axis_size("yz")
    face_side = 1 << (lane_count.bit_length() - 1) // 2
    going_up = jnp.concatenate([outgoing[0], outgoing[4], outgoing[7]], axis=0)
    going_down = jnp.concatenate([outgoing[1], outgoing[5], outgoing[6]], axis=0)
    from_left = shifted(going_up, "yz", 1).reshape(3, slot_cap, row_width)
    from_right = shifted(going_down, "yz", -1).reshape(3, slot_cap, row_width)
    from_back = shifted(outgoing[8], "gx", 1)
    from_front = shifted(outgoing[9], "gx", -1)
    upward = jnp.concatenate([outgoing[2], from_left[1], from_right[2]], axis=0)
    downward = jnp.concatenate([outgoing[3], from_left[2], from_right[1]], axis=0)
    came_up = shifted(upward, "yz", face_side).reshape(3, slot_cap, row_width)
    came_down = shifted(downward, "yz", -face_side).reshape(3, slot_cap, row_width)
    received = jnp.concatenate(
        [
            from_left[0],
            from_right[0],
            came_up[0],
            came_down[0],
            came_up[1],
            came_down[2],
            came_up[2],
            came_down[1],
            from_back,
            from_front,
        ],
        axis=0,
    )
    return finish(own_t, received, recv_list, inv_mass, basis, fields)


def solution(mesh):
    placed = (
        P(("gx", "yz"), None),
        P(),
        P(),
        P(),
        P(("gx", "yz")),
        P(("gx", "yz")),
        P(("gx", "yz")),
        P(("gx", "yz")),
        P(("gx", "yz"), None),
        P(("gx", "yz"), None),
    )
    return jax.shard_map(
        on_device, mesh=mesh, in_specs=placed, out_specs=P(("gx", "yz"), None), check_vma=False
    )
```

```python
import functools

import jax
import jax.numpy as jnp
from jax import lax
from jax.experimental import pallas as pl
from jax.experimental.pallas import tpu as pltpu
from jax.sharding import PartitionSpec as P

F32 = jnp.float32
BF16 = jnp.bfloat16


def tet_kernel(
    zone_ref, table_ref, vol_ref, dest_ref, coeff_ref, bold_ref, bnew_ref, qw_ref,
    own_ref, slot_out_ref, ct_ref, bnewt_ref, qwt_ref, slot_ref, mom_ref,
    *, tables, basis, fields, zones, slots_pad
):
    step = pl.program_id(0)
    nt = (((1,), (1,)), ((), ()))
    width = basis * fields

    @pl.when(step == 0)
    def _():
        own_ref[...] = jnp.zeros_like(own_ref)
        slot_ref[...] = jnp.zeros_like(slot_ref)
        row = lax.broadcasted_iota(jnp.int32, (width, width), 0)
        col = lax.broadcasted_iota(jnp.int32, (width, width), 1)
        shuffle = (col == (row % basis) * fields + row // basis).astype(BF16)
        ct_ref[...] = lax.dot_general(shuffle, coeff_ref[...], nt, preferred_element_type=F32).astype(BF16)
        eye = (
            lax.broadcasted_iota(jnp.int32, (basis, basis), 0) == lax.broadcasted_iota(jnp.int32, (basis, basis), 1)
        ).astype(BF16)
        for t in range(tables):
            piece = bnew_ref[t * basis : (t + 1) * basis, :]
            bnewt_ref[t * basis : (t + 1) * basis, :] = lax.dot_general(
                eye, piece, nt, preferred_element_type=F32
            ).astype(BF16)
        weights = qw_ref[...]
        high = weights.astype(BF16)
        rest = weights - high.astype(F32)
        mid = rest.astype(BF16)
        low = (rest - mid.astype(F32)).astype(BF16)
        qwt_ref[...] = (
            lax.dot_general(eye, high, nt, preferred_element_type=F32)
            + lax.dot_general(eye, mid, nt, preferred_element_type=F32)
        ) + lax.dot_general(eye, low, nt, preferred_element_type=F32)

    block = zone_ref.shape[1]
    zone = zone_ref[...]
    zone_hot = (lax.broadcasted_iota(jnp.int32, (zones, block), 0) == zone).astype(BF16)
    picked = jnp.dot(ct_ref[...], zone_hot, preferred_element_type=F32).astype(BF16)
    table = table_ref[...]
    masks = [table == t for t in range(tables)]
    qwt = qwt_ref[...]
    scale = jnp.broadcast_to(qwt[:, 0:1], (basis, block))
    for t in range(1, tables):
        scale = jnp.where(masks[t], qwt[:, t : t + 1], scale)
    scale = scale * vol_ref[...]
    bold = bold_ref[...]
    bnewt = bnewt_ref[...]
    for f in range(fields):
        every = jnp.dot(bold, picked[f * basis : (f + 1) * basis, :], preferred_element_type=F32)
        values = every[0:basis]
        for t in range(1, tables):
            values = jnp.where(masks[t], every[t * basis : (t + 1) * basis], values)
        weighted = (scale * values).astype(BF16)
        every = jnp.dot(bnewt, weighted, preferred_element_type=F32)
        moment = every[0:basis]
        for t in range(1, tables):
            moment = jnp.where(masks[t], every[t * basis : (t + 1) * basis], moment)
        mom_ref[f * basis : (f + 1) * basis, :] = moment
    moments = mom_ref[...]
    high = moments.astype(BF16)
    low = (moments - high.astype(F32)).astype(BF16)
    dest = dest_ref[...]
    own_hot = (lax.broadcasted_iota(jnp.int32, (zones, block), 0) == dest).astype(BF16)
    own_ref[...] += lax.dot_general(high, own_hot, nt, preferred_element_type=F32) + lax.dot_general(
        low, own_hot, nt, preferred_element_type=F32
    )
    slot_hot = (lax.broadcasted_iota(jnp.int32, (slots_pad, block), 0) + zones == dest).astype(BF16)
    slot_ref[...] += lax.dot_general(slot_hot, high, nt, preferred_element_type=F32) + lax.dot_general(
        slot_hot, low, nt, preferred_element_type=F32
    )

    @pl.when(step == pl.num_programs(0) - 1)
    def _():
        slot_out_ref[...] = slot_ref[...].astype(BF16)


def tet_partials(old_coeff, bold, bnew, quad_weight, zone, table, vol, dest, slots_pad, block):
    tet_count = zone.shape[0]
    zones, width = old_coeff.shape
    tables = quad_weight.shape[0]
    basis = bold.shape[1]
    fields = width // basis
    kernel = functools.partial(
        tet_kernel, tables=tables, basis=basis, fields=fields, zones=zones, slots_pad=slots_pad
    )
    row_spec = pl.BlockSpec((1, block), lambda i: (0, i))
    whole = lambda shape: pl.BlockSpec(shape, lambda i: (0, 0))
    return pl.pallas_call(
        kernel,
        grid=(tet_count // block,),
        in_specs=[
            row_spec,
            row_spec,
            row_spec,
            row_spec,
            whole(old_coeff.shape),
            whole(bold.shape),
            whole(bnew.shape),
            whole(quad_weight.shape),
        ],
        out_specs=[whole((width, zones)), whole((slots_pad, width))],
        out_shape=[
            jax.ShapeDtypeStruct((width, zones), F32),
            jax.ShapeDtypeStruct((slots_pad, width), BF16),
        ],
        scratch_shapes=[
            pltpu.VMEM((width, zones), BF16),
            pltpu.VMEM(bnew.shape, BF16),
            pltpu.VMEM((basis, tables), F32),
            pltpu.VMEM((slots_pad, width), F32),
            pltpu.VMEM((width, block), F32),
        ],
        compiler_params=pltpu.CompilerParams(dimension_semantics=("arbitrary",)),
    )(
        zone.reshape(1, tet_count),
        table.reshape(1, tet_count),
        vol.reshape(1, tet_count),
        dest.reshape(1, tet_count),
        old_coeff,
        bold,
        bnew,
        quad_weight,
    )


def finish_kernel(own_ref, recv_ref, list_ref, inv_ref, out_ref, g_ref, h_ref, invt_ref, acc_ref, *, basis, fields):
    width, zones = own_ref.shape
    slots = recv_ref.shape[0]
    slot_hot = (lax.broadcasted_iota(jnp.int32, (zones, slots), 0) == list_ref[...]).astype(F32)
    arrived = jnp.dot(slot_hot, recv_ref[...].astype(F32), preferred_element_type=F32)
    rounded = (own_ref[...] + arrived.T).astype(BF16).astype(F32)
    lanes = 128
    halves = zones // lanes
    for half in range(halves):
        g_ref[half * width : (half + 1) * width, :] = rounded[:, half * lanes : (half + 1) * lanes]
    for k in range(basis):
        for half in range(halves):
            h_ref[k * fields : (k + 1) * fields, half * lanes : (half + 1) * lanes] = g_ref[
                pl.ds(half * width + k, fields, stride=basis), :
            ]
    chunk = 128
    for c in range(basis * basis // chunk):
        invt_ref[c * chunk : (c + 1) * chunk, :] = inv_ref[:, c * chunk : (c + 1) * chunk].astype(F32).T

    def body(j, carry):
        acc = jnp.zeros((fields, zones), F32)
        for k in range(basis):
            acc = acc + invt_ref[pl.ds(j * basis + k, 1), :] * h_ref[k * fields : (k + 1) * fields, :]
        acc_ref[pl.ds(pl.multiple_of(j * fields, fields), fields), :] = acc
        return carry

    lax.fori_loop(0, basis, body, 0)
    out_ref[...] = acc_ref[...].T


def finish(own_t, received, recv_row, inv_mass, basis, fields):
    width, zones = own_t.shape
    kernel = functools.partial(finish_kernel, basis=basis, fields=fields)
    return pl.pallas_call(
        kernel,
        out_shape=jax.ShapeDtypeStruct((zones, width), F32),
        scratch_shapes=[
            pltpu.VMEM((zones // 128 * width, 128), F32),
            pltpu.VMEM((width, zones), F32),
            pltpu.VMEM((basis * basis, zones), F32),
            pltpu.VMEM((width, zones), F32),
        ],
    )(own_t, received, recv_row, inv_mass)


def shifted(block, axis, distance):
    count = lax.axis_size(axis)
    route = [(i, (i + distance) % count) for i in range(count)]
    return lax.ppermute(block, axis, route)


def on_device(
    old_coeff,
    basis_old,
    basis_new,
    quad_weight,
    tet_zone,
    tet_table,
    tet_volume,
    tet_dest,
    recv_list,
    inv_mass,
):
    zone_count, row_width = old_coeff.shape
    tables, quad, basis = basis_old.shape
    fields = row_width // basis
    slot_total = recv_list.shape[1]
    partner_count = 10
    slot_cap = slot_total // partner_count
    slots_pad = -(-slot_total // 128) * 128
    block = min(512, tet_zone.shape[0])

    bold = basis_old.reshape(tables * quad, basis)
    bnew = basis_new.reshape(tables * quad, basis)
    own_t, slot_rows = tet_partials(
        old_coeff, bold, bnew, quad_weight, tet_zone, tet_table, tet_volume, tet_dest, slots_pad, block
    )
    outgoing = slot_rows[:slot_total].reshape(partner_count, slot_cap, row_width)

    lane_count = lax.axis_size("yz")
    face_side = 1 << (lane_count.bit_length() - 1) // 2
    going_up = jnp.concatenate([outgoing[0], outgoing[4], outgoing[7]], axis=0)
    going_down = jnp.concatenate([outgoing[1], outgoing[5], outgoing[6]], axis=0)
    from_left = shifted(going_up, "yz", 1).reshape(3, slot_cap, row_width)
    from_right = shifted(going_down, "yz", -1).reshape(3, slot_cap, row_width)
    from_back = shifted(outgoing[8], "gx", 1)
    from_front = shifted(outgoing[9], "gx", -1)
    upward = jnp.concatenate([outgoing[2], from_left[1], from_right[2]], axis=0)
    downward = jnp.concatenate([outgoing[3], from_left[2], from_right[1]], axis=0)
    came_up = shifted(upward, "yz", face_side).reshape(3, slot_cap, row_width)
    came_down = shifted(downward, "yz", -face_side).reshape(3, slot_cap, row_width)
    received = jnp.concatenate(
        [
            from_left[0],
            from_right[0],
            came_up[0],
            came_down[0],
            came_up[1],
            came_down[2],
            came_up[2],
            came_down[1],
            from_back,
            from_front,
        ],
        axis=0,
    )
    return finish(own_t, received, recv_list, inv_mass, basis, fields)


def solution(mesh):
    placed = (
        P(("gx", "yz"), None),
        P(),
        P(),
        P(),
        P(("gx", "yz")),
        P(("gx", "yz")),
        P(("gx", "yz")),
        P(("gx", "yz")),
        P(("gx", "yz"), None),
        P(("gx", "yz"), None),
    )
    return jax.shard_map(
        on_device, mesh=mesh, in_specs=placed, out_specs=P(("gx", "yz"), None), check_vma=False
    )
```

```python
import functools

import jax
import jax.numpy as jnp
from jax import lax
from jax.experimental import pallas as pl
from jax.experimental.pallas import tpu as pltpu
from jax.sharding import PartitionSpec as P

F32 = jnp.float32
BF16 = jnp.bfloat16


def tet_kernel(
    zone_ref, table_ref, vol_ref, dest_ref, coeff_ref, bold_ref, bnew_ref, qw_ref,
    own_ref, slot_out_ref, ct_ref, boldc_ref, bnewc_ref, qwt_ref, slot_ref, mom_ref, spread_ref,
    *, tables, basis, fields, zones, slots_pad
):
    step = pl.program_id(0)
    nt = (((1,), (1,)), ((), ()))
    width = basis * fields

    @pl.when(step == 0)
    def _():
        own_ref[...] = jnp.zeros_like(own_ref)
        slot_ref[...] = jnp.zeros_like(slot_ref)
        row = lax.broadcasted_iota(jnp.int32, (width, width), 0)
        col = lax.broadcasted_iota(jnp.int32, (width, width), 1)
        shuffle = (col == (row % basis) * fields + row // basis).astype(BF16)
        ct_ref[...] = lax.dot_general(shuffle, coeff_ref[...], nt, preferred_element_type=F32).astype(BF16)
        eye = (
            lax.broadcasted_iota(jnp.int32, (basis, basis), 0) == lax.broadcasted_iota(jnp.int32, (basis, basis), 1)
        ).astype(BF16)
        for t in range(tables):
            boldc_ref[:, t * basis : (t + 1) * basis] = bold_ref[t * basis : (t + 1) * basis, :]
            piece = bnew_ref[t * basis : (t + 1) * basis, :]
            bnewc_ref[:, t * basis : (t + 1) * basis] = lax.dot_general(
                eye, piece, nt, preferred_element_type=F32
            ).astype(BF16)
        weights = qw_ref[...]
        high = weights.astype(BF16)
        rest = weights - high.astype(F32)
        mid = rest.astype(BF16)
        low = (rest - mid.astype(F32)).astype(BF16)
        qwt_ref[...] = (
            lax.dot_general(eye, high, nt, preferred_element_type=F32)
            + lax.dot_general(eye, mid, nt, preferred_element_type=F32)
        ) + lax.dot_general(eye, low, nt, preferred_element_type=F32)

    block = zone_ref.shape[1]
    zone = zone_ref[...]
    zone_hot = (lax.broadcasted_iota(jnp.int32, (zones, block), 0) == zone).astype(BF16)
    picked = jnp.dot(ct_ref[...], zone_hot, preferred_element_type=F32).astype(BF16)
    table = table_ref[...]
    masks = [table == t for t in range(tables)]
    qwt = qwt_ref[...]
    scale = jnp.broadcast_to(qwt[:, 0:1], (basis, block))
    for t in range(1, tables):
        scale = jnp.where(masks[t], qwt[:, t : t + 1], scale)
    scale = scale * vol_ref[...]
    boldc = boldc_ref[...]
    bnewc = bnewc_ref[...]
    empty = jnp.zeros((basis, block), BF16)
    for f in range(fields):
        piece = picked[f * basis : (f + 1) * basis, :]
        for t in range(tables):
            spread_ref[t * basis : (t + 1) * basis, :] = jnp.where(masks[t], piece, empty)
        values = jnp.dot(boldc, spread_ref[...], preferred_element_type=F32)
        weighted = (scale * values).astype(BF16)
        for t in range(tables):
            spread_ref[t * basis : (t + 1) * basis, :] = jnp.where(masks[t], weighted, empty)
        mom_ref[f * basis : (f + 1) * basis, :] = jnp.dot(bnewc, spread_ref[...], preferred_element_type=F32)
    moments = mom_ref[...]
    high = moments.astype(BF16)
    low = (moments - high.astype(F32)).astype(BF16)
    dest = dest_ref[...]
    own_hot = (lax.broadcasted_iota(jnp.int32, (zones, block), 0) == dest).astype(BF16)
    own_ref[...] += lax.dot_general(high, own_hot, nt, preferred_element_type=F32) + lax.dot_general(
        low, own_hot, nt, preferred_element_type=F32
    )
    slot_hot = (lax.broadcasted_iota(jnp.int32, (slots_pad, block), 0) + zones == dest).astype(BF16)
    slot_ref[...] += lax.dot_general(slot_hot, high, nt, preferred_element_type=F32) + lax.dot_general(
        slot_hot, low, nt, preferred_element_type=F32
    )

    @pl.when(step == pl.num_programs(0) - 1)
    def _():
        slot_out_ref[...] = slot_ref[...].astype(BF16)


def tet_partials(old_coeff, bold, bnew, quad_weight, zone, table, vol, dest, slots_pad, block):
    tet_count = zone.shape[0]
    zones, width = old_coeff.shape
    tables = quad_weight.shape[0]
    basis = bold.shape[1]
    fields = width // basis
    kernel = functools.partial(
        tet_kernel, tables=tables, basis=basis, fields=fields, zones=zones, slots_pad=slots_pad
    )
    row_spec = pl.BlockSpec((1, block), lambda i: (0, i))
    whole = lambda shape: pl.BlockSpec(shape, lambda i: (0, 0))
    return pl.pallas_call(
        kernel,
        grid=(tet_count // block,),
        in_specs=[
            row_spec,
            row_spec,
            row_spec,
            row_spec,
            whole(old_coeff.shape),
            whole(bold.shape),
            whole(bnew.shape),
            whole(quad_weight.shape),
        ],
        out_specs=[whole((width, zones)), whole((slots_pad, width))],
        out_shape=[
            jax.ShapeDtypeStruct((width, zones), F32),
            jax.ShapeDtypeStruct((slots_pad, width), BF16),
        ],
        scratch_shapes=[
            pltpu.VMEM((width, zones), BF16),
            pltpu.VMEM((basis, tables * basis), BF16),
            pltpu.VMEM((basis, tables * basis), BF16),
            pltpu.VMEM((basis, tables), F32),
            pltpu.VMEM((slots_pad, width), F32),
            pltpu.VMEM((width, block), F32),
            pltpu.VMEM((tables * basis, block), BF16),
        ],
        compiler_params=pltpu.CompilerParams(dimension_semantics=("arbitrary",)),
    )(
        zone.reshape(1, tet_count),
        table.reshape(1, tet_count),
        vol.reshape(1, tet_count),
        dest.reshape(1, tet_count),
        old_coeff,
        bold,
        bnew,
        quad_weight,
    )


def finish_kernel(own_ref, recv_ref, list_ref, inv_ref, out_ref, g_ref, h_ref, invt_ref, acc_ref, *, basis, fields):
    width, zones = own_ref.shape
    slots = recv_ref.shape[0]
    slot_hot = (lax.broadcasted_iota(jnp.int32, (zones, slots), 0) == list_ref[...]).astype(F32)
    arrived = jnp.dot(slot_hot, recv_ref[...].astype(F32), preferred_element_type=F32)
    rounded = (own_ref[...] + arrived.T).astype(BF16).astype(F32)
    lanes = 128
    halves = zones // lanes
    for half in range(halves):
        g_ref[half * width : (half + 1) * width, :] = rounded[:, half * lanes : (half + 1) * lanes]
    for k in range(basis):
        for half in range(halves):
            h_ref[k * fields : (k + 1) * fields, half * lanes : (half + 1) * lanes] = g_ref[
                pl.ds(half * width + k, fields, stride=basis), :
            ]
    chunk = 128
    for c in range(basis * basis // chunk):
        invt_ref[c * chunk : (c + 1) * chunk, :] = inv_ref[:, c * chunk : (c + 1) * chunk].astype(F32).T

    def body(j, carry):
        acc = jnp.zeros((fields, zones), F32)
        for k in range(basis):
            acc = acc + invt_ref[pl.ds(j * basis + k, 1), :] * h_ref[k * fields : (k + 1) * fields, :]
        acc_ref[pl.ds(pl.multiple_of(j * fields, fields), fields), :] = acc
        return carry

    lax.fori_loop(0, basis, body, 0)
    out_ref[...] = acc_ref[...].T


def finish(own_t, received, recv_row, inv_mass, basis, fields):
    width, zones = own_t.shape
    kernel = functools.partial(finish_kernel, basis=basis, fields=fields)
    return pl.pallas_call(
        kernel,
        out_shape=jax.ShapeDtypeStruct((zones, width), F32),
        scratch_shapes=[
            pltpu.VMEM((zones // 128 * width, 128), F32),
            pltpu.VMEM((width, zones), F32),
            pltpu.VMEM((basis * basis, zones), F32),
            pltpu.VMEM((width, zones), F32),
        ],
    )(own_t, received, recv_row, inv_mass)


def shifted(block, axis, distance):
    count = lax.axis_size(axis)
    route = [(i, (i + distance) % count) for i in range(count)]
    return lax.ppermute(block, axis, route)


def on_device(
    old_coeff,
    basis_old,
    basis_new,
    quad_weight,
    tet_zone,
    tet_table,
    tet_volume,
    tet_dest,
    recv_list,
    inv_mass,
):
    zone_count, row_width = old_coeff.shape
    tables, quad, basis = basis_old.shape
    fields = row_width // basis
    slot_total = recv_list.shape[1]
    partner_count = 10
    slot_cap = slot_total // partner_count
    slots_pad = -(-slot_total // 128) * 128
    block = min(512, tet_zone.shape[0])

    bold = basis_old.reshape(tables * quad, basis)
    bnew = basis_new.reshape(tables * quad, basis)
    own_t, slot_rows = tet_partials(
        old_coeff, bold, bnew, quad_weight, tet_zone, tet_table, tet_volume, tet_dest, slots_pad, block
    )
    outgoing = slot_rows[:slot_total].reshape(partner_count, slot_cap, row_width)

    lane_count = lax.axis_size("yz")
    face_side = 1 << (lane_count.bit_length() - 1) // 2
    going_up = jnp.concatenate([outgoing[0], outgoing[4], outgoing[7]], axis=0)
    going_down = jnp.concatenate([outgoing[1], outgoing[5], outgoing[6]], axis=0)
    from_left = shifted(going_up, "yz", 1).reshape(3, slot_cap, row_width)
    from_right = shifted(going_down, "yz", -1).reshape(3, slot_cap, row_width)
    from_back = shifted(outgoing[8], "gx", 1)
    from_front = shifted(outgoing[9], "gx", -1)
    upward = jnp.concatenate([outgoing[2], from_left[1], from_right[2]], axis=0)
    downward = jnp.concatenate([outgoing[3], from_left[2], from_right[1]], axis=0)
    came_up = shifted(upward, "yz", face_side).reshape(3, slot_cap, row_width)
    came_down = shifted(downward, "yz", -face_side).reshape(3, slot_cap, row_width)
    received = jnp.concatenate(
        [
            from_left[0],
            from_right[0],
            came_up[0],
            came_down[0],
            came_up[1],
            came_down[2],
            came_up[2],
            came_down[1],
            from_back,
            from_front,
        ],
        axis=0,
    )
    return finish(own_t, received, recv_list, inv_mass, basis, fields)


def solution(mesh):
    placed = (
        P(("gx", "yz"), None),
        P(),
        P(),
        P(),
        P(("gx", "yz")),
        P(("gx", "yz")),
        P(("gx", "yz")),
        P(("gx", "yz")),
        P(("gx", "yz"), None),
        P(("gx", "yz"), None),
    )
    return jax.shard_map(
        on_device, mesh=mesh, in_specs=placed, out_specs=P(("gx", "yz"), None), check_vma=False
    )
```

```python
import functools

import jax
import jax.numpy as jnp
from jax import lax
from jax.experimental import pallas as pl
from jax.experimental.pallas import tpu as pltpu
from jax.sharding import PartitionSpec as P

F32 = jnp.float32
BF16 = jnp.bfloat16


def tet_kernel(
    zone_ref, table_ref, vol_ref, dest_ref, coeff_ref, bold_ref, bnew_ref, qw_ref,
    own_ref, slot_out_ref, ct_ref, boldc_ref, bnewc_ref, qwt_ref, slot_ref, mom_ref, spread_ref,
    *, tables, basis, fields, zones, slots_pad
):
    step = pl.program_id(0)
    nt = (((1,), (1,)), ((), ()))
    width = basis * fields

    @pl.when(step == 0)
    def _():
        own_ref[...] = jnp.zeros_like(own_ref)
        slot_ref[...] = jnp.zeros_like(slot_ref)
        row = lax.broadcasted_iota(jnp.int32, (width, width), 0)
        col = lax.broadcasted_iota(jnp.int32, (width, width), 1)
        shuffle = (col == (row % basis) * fields + row // basis).astype(BF16)
        ct_ref[...] = lax.dot_general(shuffle, coeff_ref[...], nt, preferred_element_type=F32).astype(BF16)
        eye = (
            lax.broadcasted_iota(jnp.int32, (basis, basis), 0) == lax.broadcasted_iota(jnp.int32, (basis, basis), 1)
        ).astype(BF16)
        for t in range(tables):
            boldc_ref[:, t * basis : (t + 1) * basis] = bold_ref[t * basis : (t + 1) * basis, :]
            piece = bnew_ref[t * basis : (t + 1) * basis, :]
            bnewc_ref[:, t * basis : (t + 1) * basis] = lax.dot_general(
                eye, piece, nt, preferred_element_type=F32
            ).astype(BF16)
        weights = qw_ref[...]
        high = weights.astype(BF16)
        rest = weights - high.astype(F32)
        mid = rest.astype(BF16)
        low = (rest - mid.astype(F32)).astype(BF16)
        qwt_ref[...] = (
            lax.dot_general(eye, high, nt, preferred_element_type=F32)
            + lax.dot_general(eye, mid, nt, preferred_element_type=F32)
        ) + lax.dot_general(eye, low, nt, preferred_element_type=F32)

    block = zone_ref.shape[1]
    zone = zone_ref[...]
    zone_hot = (lax.broadcasted_iota(jnp.int32, (zones, block), 0) == zone).astype(BF16)
    picked = jnp.dot(ct_ref[...], zone_hot, preferred_element_type=F32).astype(BF16)
    table = table_ref[...]
    masks = [table == t for t in range(tables)]
    qwt = qwt_ref[...]
    scale = jnp.broadcast_to(qwt[:, 0:1], (basis, block))
    for t in range(1, tables):
        scale = jnp.where(masks[t], qwt[:, t : t + 1], scale)
    scale = scale * vol_ref[...]
    boldc = boldc_ref[...]
    bnewc = bnewc_ref[...]
    empty = jnp.zeros((basis, block), BF16)
    for f in range(fields):
        piece = picked[f * basis : (f + 1) * basis, :]
        for t in range(tables):
            spread_ref[t * basis : (t + 1) * basis, :] = jnp.where(masks[t], piece, empty)
        values = jnp.dot(boldc, spread_ref[...], preferred_element_type=F32)
        weighted = (scale * values).astype(BF16)
        for t in range(tables):
            spread_ref[t * basis : (t + 1) * basis, :] = jnp.where(masks[t], weighted, empty)
        mom_ref[f * basis : (f + 1) * basis, :] = jnp.dot(bnewc, spread_ref[...], preferred_element_type=F32)
    moments = mom_ref[...]
    high = moments.astype(BF16)
    low = (moments - high.astype(F32)).astype(BF16)
    dest = dest_ref[...]
    own_hot = (lax.broadcasted_iota(jnp.int32, (zones, block), 0) == dest).astype(BF16)
    own_ref[...] += lax.dot_general(high, own_hot, nt, preferred_element_type=F32) + lax.dot_general(
        low, own_hot, nt, preferred_element_type=F32
    )
    slot_hot = (lax.broadcasted_iota(jnp.int32, (slots_pad, block), 0) + zones == dest).astype(BF16)
    slot_ref[...] += lax.dot_general(slot_hot, high, nt, preferred_element_type=F32) + lax.dot_general(
        slot_hot, low, nt, preferred_element_type=F32
    )

    @pl.when(step == pl.num_programs(0) - 1)
    def _():
        slot_out_ref[...] = slot_ref[...].astype(BF16)


def tet_partials(old_coeff, bold, bnew, quad_weight, zone, table, vol, dest, slots_pad, block):
    tet_count = zone.shape[0]
    zones, width = old_coeff.shape
    tables = quad_weight.shape[0]
    basis = bold.shape[1]
    fields = width // basis
    kernel = functools.partial(
        tet_kernel, tables=tables, basis=basis, fields=fields, zones=zones, slots_pad=slots_pad
    )
    row_spec = pl.BlockSpec((1, block), lambda i: (0, i))
    whole = lambda shape: pl.BlockSpec(shape, lambda i: (0, 0))
    return pl.pallas_call(
        kernel,
        grid=(tet_count // block,),
        in_specs=[
            row_spec,
            row_spec,
            row_spec,
            row_spec,
            whole(old_coeff.shape),
            whole(bold.shape),
            whole(bnew.shape),
            whole(quad_weight.shape),
        ],
        out_specs=[whole((width, zones)), whole((slots_pad, width))],
        out_shape=[
            jax.ShapeDtypeStruct((width, zones), F32),
            jax.ShapeDtypeStruct((slots_pad, width), BF16),
        ],
        scratch_shapes=[
            pltpu.VMEM((width, zones), BF16),
            pltpu.VMEM((basis, tables * basis), BF16),
            pltpu.VMEM((basis, tables * basis), BF16),
            pltpu.VMEM((basis, tables), F32),
            pltpu.VMEM((slots_pad, width), F32),
            pltpu.VMEM((width, block), F32),
            pltpu.VMEM((tables * basis, block), BF16),
        ],
        compiler_params=pltpu.CompilerParams(dimension_semantics=("arbitrary",)),
    )(
        zone.reshape(1, tet_count),
        table.reshape(1, tet_count),
        vol.reshape(1, tet_count),
        dest.reshape(1, tet_count),
        old_coeff,
        bold,
        bnew,
        quad_weight,
    )


def finish_kernel(own_ref, recv_ref, list_ref, inv_ref, out_ref, g_ref, h_ref, invt_ref, acc_ref, *, basis, fields):
    width, zones = own_ref.shape
    slots = recv_ref.shape[0]
    slot_hot = (lax.broadcasted_iota(jnp.int32, (zones, slots), 0) == list_ref[...]).astype(F32)
    arrived = jnp.dot(slot_hot, recv_ref[...].astype(F32), preferred_element_type=F32)
    rounded = (own_ref[...] + arrived.T).astype(BF16).astype(F32)
    lanes = 128
    halves = zones // lanes
    for half in range(halves):
        g_ref[half * width : (half + 1) * width, :] = rounded[:, half * lanes : (half + 1) * lanes]
    for k in range(basis):
        for half in range(halves):
            h_ref[k * fields : (k + 1) * fields, half * lanes : (half + 1) * lanes] = g_ref[
                pl.ds(half * width + k, fields, stride=basis), :
            ]
    chunk = 128
    for c in range(basis * basis // chunk):
        invt_ref[c * chunk : (c + 1) * chunk, :] = inv_ref[:, c * chunk : (c + 1) * chunk].astype(F32).T

    chains = 8

    def body(j, carry):
        sums = [jnp.zeros((fields, zones), F32) for _ in range(chains)]
        for k in range(basis):
            sums[k % chains] = (
                sums[k % chains] + invt_ref[pl.ds(j * basis + k, 1), :] * h_ref[k * fields : (k + 1) * fields, :]
            )
        while len(sums) > 1:
            sums = [sums[i] + sums[i + 1] for i in range(0, len(sums), 2)]
        acc_ref[pl.ds(pl.multiple_of(j * fields, fields), fields), :] = sums[0]
        return carry

    lax.fori_loop(0, basis, body, 0)
    out_ref[...] = acc_ref[...].T


def finish(own_t, received, recv_row, inv_mass, basis, fields):
    width, zones = own_t.shape
    kernel = functools.partial(finish_kernel, basis=basis, fields=fields)
    return pl.pallas_call(
        kernel,
        out_shape=jax.ShapeDtypeStruct((zones, width), F32),
        scratch_shapes=[
            pltpu.VMEM((zones // 128 * width, 128), F32),
            pltpu.VMEM((width, zones), F32),
            pltpu.VMEM((basis * basis, zones), F32),
            pltpu.VMEM((width, zones), F32),
        ],
    )(own_t, received, recv_row, inv_mass)


def shifted(block, axis, distance):
    count = lax.axis_size(axis)
    route = [(i, (i + distance) % count) for i in range(count)]
    return lax.ppermute(block, axis, route)


def on_device(
    old_coeff,
    basis_old,
    basis_new,
    quad_weight,
    tet_zone,
    tet_table,
    tet_volume,
    tet_dest,
    recv_list,
    inv_mass,
):
    zone_count, row_width = old_coeff.shape
    tables, quad, basis = basis_old.shape
    fields = row_width // basis
    slot_total = recv_list.shape[1]
    partner_count = 10
    slot_cap = slot_total // partner_count
    slots_pad = -(-slot_total // 128) * 128
    block = min(512, tet_zone.shape[0])

    bold = basis_old.reshape(tables * quad, basis)
    bnew = basis_new.reshape(tables * quad, basis)
    own_t, slot_rows = tet_partials(
        old_coeff, bold, bnew, quad_weight, tet_zone, tet_table, tet_volume, tet_dest, slots_pad, block
    )
    outgoing = slot_rows[:slot_total].reshape(partner_count, slot_cap, row_width)

    lane_count = lax.axis_size("yz")
    face_side = 1 << (lane_count.bit_length() - 1) // 2
    going_up = jnp.concatenate([outgoing[0], outgoing[4], outgoing[7]], axis=0)
    going_down = jnp.concatenate([outgoing[1], outgoing[5], outgoing[6]], axis=0)
    from_left = shifted(going_up, "yz", 1).reshape(3, slot_cap, row_width)
    from_right = shifted(going_down, "yz", -1).reshape(3, slot_cap, row_width)
    from_back = shifted(outgoing[8], "gx", 1)
    from_front = shifted(outgoing[9], "gx", -1)
    upward = jnp.concatenate([outgoing[2], from_left[1], from_right[2]], axis=0)
    downward = jnp.concatenate([outgoing[3], from_left[2], from_right[1]], axis=0)
    came_up = shifted(upward, "yz", face_side).reshape(3, slot_cap, row_width)
    came_down = shifted(downward, "yz", -face_side).reshape(3, slot_cap, row_width)
    received = jnp.concatenate(
        [
            from_left[0],
            from_right[0],
            came_up[0],
            came_down[0],
            came_up[1],
            came_down[2],
            came_up[2],
            came_down[1],
            from_back,
            from_front,
        ],
        axis=0,
    )
    return finish(own_t, received, recv_list, inv_mass, basis, fields)


def solution(mesh):
    placed = (
        P(("gx", "yz"), None),
        P(),
        P(),
        P(),
        P(("gx", "yz")),
        P(("gx", "yz")),
        P(("gx", "yz")),
        P(("gx", "yz")),
        P(("gx", "yz"), None),
        P(("gx", "yz"), None),
    )
    return jax.shard_map(
        on_device, mesh=mesh, in_specs=placed, out_specs=P(("gx", "yz"), None), check_vma=False
    )
```

```python
import functools

import jax
import jax.numpy as jnp
from jax import lax
from jax.experimental import pallas as pl
from jax.experimental.pallas import tpu as pltpu
from jax.sharding import PartitionSpec as P

F32 = jnp.float32
BF16 = jnp.bfloat16


def tet_kernel(
    zone_ref, table_ref, vol_ref, dest_ref, coeff_ref, bold_ref, bnew_ref, qw_ref,
    own_ref, slot_out_ref, ct_ref, boldc_ref, bnewc_ref, qwt_ref, slot_ref, mom_ref, spread_ref,
    *, tables, basis, fields, zones, slots_pad
):
    step = pl.program_id(0)
    nt = (((1,), (1,)), ((), ()))
    width = basis * fields

    @pl.when(step == 0)
    def _():
        own_ref[...] = jnp.zeros_like(own_ref)
        slot_ref[...] = jnp.zeros_like(slot_ref)
        row = lax.broadcasted_iota(jnp.int32, (width, width), 0)
        col = lax.broadcasted_iota(jnp.int32, (width, width), 1)
        shuffle = (col == (row % basis) * fields + row // basis).astype(BF16)
        ct_ref[...] = lax.dot_general(shuffle, coeff_ref[...], nt, preferred_element_type=F32).astype(BF16)
        eye = (
            lax.broadcasted_iota(jnp.int32, (basis, basis), 0) == lax.broadcasted_iota(jnp.int32, (basis, basis), 1)
        ).astype(BF16)
        for t in range(tables):
            boldc_ref[:, t * basis : (t + 1) * basis] = bold_ref[t * basis : (t + 1) * basis, :]
            piece = bnew_ref[t * basis : (t + 1) * basis, :]
            bnewc_ref[:, t * basis : (t + 1) * basis] = lax.dot_general(
                eye, piece, nt, preferred_element_type=F32
            ).astype(BF16)
        weights = qw_ref[...]
        high = weights.astype(BF16)
        rest = weights - high.astype(F32)
        mid = rest.astype(BF16)
        low = (rest - mid.astype(F32)).astype(BF16)
        qwt_ref[...] = (
            lax.dot_general(eye, high, nt, preferred_element_type=F32)
            + lax.dot_general(eye, mid, nt, preferred_element_type=F32)
        ) + lax.dot_general(eye, low, nt, preferred_element_type=F32)

    block = zone_ref.shape[1]
    zone = zone_ref[...]
    zone_hot = (lax.broadcasted_iota(jnp.int32, (zones, block), 0) == zone).astype(BF16)
    picked = jnp.dot(ct_ref[...], zone_hot, preferred_element_type=F32).astype(BF16)
    table = table_ref[...]
    masks = [table == t for t in range(tables)]
    qwt = qwt_ref[...]
    scale = jnp.broadcast_to(qwt[:, 0:1], (basis, block))
    for t in range(1, tables):
        scale = jnp.where(masks[t], qwt[:, t : t + 1], scale)
    scale = scale * vol_ref[...]
    boldc = boldc_ref[...]
    bnewc = bnewc_ref[...]
    empty = jnp.zeros((basis, block), BF16)
    for f in range(fields):
        piece = picked[f * basis : (f + 1) * basis, :]
        for t in range(tables):
            spread_ref[t * basis : (t + 1) * basis, :] = jnp.where(masks[t], piece, empty)
        values = jnp.dot(boldc, spread_ref[...], preferred_element_type=F32)
        weighted = (scale * values).astype(BF16)
        for t in range(tables):
            spread_ref[t * basis : (t + 1) * basis, :] = jnp.where(masks[t], weighted, empty)
        mom_ref[f * basis : (f + 1) * basis, :] = jnp.dot(bnewc, spread_ref[...], preferred_element_type=F32)
    moments = mom_ref[...]
    high = moments.astype(BF16)
    low = (moments - high.astype(F32)).astype(BF16)
    dest = dest_ref[...]
    own_hot = (lax.broadcasted_iota(jnp.int32, (zones, block), 0) == dest).astype(BF16)
    own_ref[...] += lax.dot_general(high, own_hot, nt, preferred_element_type=F32) + lax.dot_general(
        low, own_hot, nt, preferred_element_type=F32
    )
    slot_hot = (lax.broadcasted_iota(jnp.int32, (slots_pad, block), 0) + zones == dest).astype(BF16)
    slot_ref[...] += lax.dot_general(slot_hot, high, nt, preferred_element_type=F32) + lax.dot_general(
        slot_hot, low, nt, preferred_element_type=F32
    )

    @pl.when(step == pl.num_programs(0) - 1)
    def _():
        slot_out_ref[...] = slot_ref[...].astype(BF16)


def tet_partials(old_coeff, bold, bnew, quad_weight, zone, table, vol, dest, slots_pad, block):
    tet_count = zone.shape[0]
    zones, width = old_coeff.shape
    tables = quad_weight.shape[0]
    basis = bold.shape[1]
    fields = width // basis
    kernel = functools.partial(
        tet_kernel, tables=tables, basis=basis, fields=fields, zones=zones, slots_pad=slots_pad
    )
    row_spec = pl.BlockSpec((1, block), lambda i: (0, i))
    whole = lambda shape: pl.BlockSpec(shape, lambda i: (0, 0))
    return pl.pallas_call(
        kernel,
        grid=(tet_count // block,),
        in_specs=[
            row_spec,
            row_spec,
            row_spec,
            row_spec,
            whole(old_coeff.shape),
            whole(bold.shape),
            whole(bnew.shape),
            whole(quad_weight.shape),
        ],
        out_specs=[whole((width, zones)), whole((slots_pad, width))],
        out_shape=[
            jax.ShapeDtypeStruct((width, zones), F32),
            jax.ShapeDtypeStruct((slots_pad, width), BF16),
        ],
        scratch_shapes=[
            pltpu.VMEM((width, zones), BF16),
            pltpu.VMEM((basis, tables * basis), BF16),
            pltpu.VMEM((basis, tables * basis), BF16),
            pltpu.VMEM((basis, tables), F32),
            pltpu.VMEM((slots_pad, width), F32),
            pltpu.VMEM((width, block), F32),
            pltpu.VMEM((tables * basis, block), BF16),
        ],
        compiler_params=pltpu.CompilerParams(dimension_semantics=("arbitrary",)),
    )(
        zone.reshape(1, tet_count),
        table.reshape(1, tet_count),
        vol.reshape(1, tet_count),
        dest.reshape(1, tet_count),
        old_coeff,
        bold,
        bnew,
        quad_weight,
    )


def finish_kernel(own_ref, recv_ref, list_ref, inv_ref, out_ref, g_ref, h_ref, invt_ref, acc_ref, *, basis, fields):
    width, zones = own_ref.shape
    slots = recv_ref.shape[0]
    slot_hot = (lax.broadcasted_iota(jnp.int32, (zones, slots), 0) == list_ref[...]).astype(F32)
    arrived = jnp.dot(slot_hot, recv_ref[...].astype(F32), preferred_element_type=F32)
    rounded = (own_ref[...] + arrived.T).astype(BF16).astype(F32)
    lanes = 128
    halves = zones // lanes
    for half in range(halves):
        g_ref[half * width : (half + 1) * width, :] = rounded[:, half * lanes : (half + 1) * lanes]
    for k in range(basis):
        for half in range(halves):
            h_ref[k * fields : (k + 1) * fields, half * lanes : (half + 1) * lanes] = g_ref[
                pl.ds(half * width + k, fields, stride=basis), :
            ]
    chunk = 128
    for c in range(basis * basis // chunk):
        invt_ref[c * chunk : (c + 1) * chunk, :] = inv_ref[:, c * chunk : (c + 1) * chunk].astype(F32).T

    chains = 8

    def body(j, carry):
        rows = invt_ref.at[pl.ds(pl.multiple_of(j * basis, basis), basis), :]
        sums = [jnp.zeros((fields, zones), F32) for _ in range(chains)]
        for k in range(basis):
            sums[k % chains] = sums[k % chains] + rows[k : k + 1, :] * h_ref[k * fields : (k + 1) * fields, :]
        while len(sums) > 1:
            sums = [sums[i] + sums[i + 1] for i in range(0, len(sums), 2)]
        acc_ref[pl.ds(pl.multiple_of(j * fields, fields), fields), :] = sums[0]
        return carry

    lax.fori_loop(0, basis, body, 0)
    out_ref[...] = acc_ref[...].T


def finish(own_t, received, recv_row, inv_mass, basis, fields):
    width, zones = own_t.shape
    kernel = functools.partial(finish_kernel, basis=basis, fields=fields)
    return pl.pallas_call(
        kernel,
        out_shape=jax.ShapeDtypeStruct((zones, width), F32),
        scratch_shapes=[
            pltpu.VMEM((zones // 128 * width, 128), F32),
            pltpu.VMEM((width, zones), F32),
            pltpu.VMEM((basis * basis, zones), F32),
            pltpu.VMEM((width, zones), F32),
        ],
    )(own_t, received, recv_row, inv_mass)


def shifted(block, axis, distance):
    count = lax.axis_size(axis)
    route = [(i, (i + distance) % count) for i in range(count)]
    return lax.ppermute(block, axis, route)


def on_device(
    old_coeff,
    basis_old,
    basis_new,
    quad_weight,
    tet_zone,
    tet_table,
    tet_volume,
    tet_dest,
    recv_list,
    inv_mass,
):
    zone_count, row_width = old_coeff.shape
    tables, quad, basis = basis_old.shape
    fields = row_width // basis
    slot_total = recv_list.shape[1]
    partner_count = 10
    slot_cap = slot_total // partner_count
    slots_pad = -(-slot_total // 128) * 128
    block = min(512, tet_zone.shape[0])

    bold = basis_old.reshape(tables * quad, basis)
    bnew = basis_new.reshape(tables * quad, basis)
    own_t, slot_rows = tet_partials(
        old_coeff, bold, bnew, quad_weight, tet_zone, tet_table, tet_volume, tet_dest, slots_pad, block
    )
    outgoing = slot_rows[:slot_total].reshape(partner_count, slot_cap, row_width)

    lane_count = lax.axis_size("yz")
    face_side = 1 << (lane_count.bit_length() - 1) // 2
    going_up = jnp.concatenate([outgoing[0], outgoing[4], outgoing[7]], axis=0)
    going_down = jnp.concatenate([outgoing[1], outgoing[5], outgoing[6]], axis=0)
    from_left = shifted(going_up, "yz", 1).reshape(3, slot_cap, row_width)
    from_right = shifted(going_down, "yz", -1).reshape(3, slot_cap, row_width)
    from_back = shifted(outgoing[8], "gx", 1)
    from_front = shifted(outgoing[9], "gx", -1)
    upward = jnp.concatenate([outgoing[2], from_left[1], from_right[2]], axis=0)
    downward = jnp.concatenate([outgoing[3], from_left[2], from_right[1]], axis=0)
    came_up = shifted(upward, "yz", face_side).reshape(3, slot_cap, row_width)
    came_down = shifted(downward, "yz", -face_side).reshape(3, slot_cap, row_width)
    received = jnp.concatenate(
        [
            from_left[0],
            from_right[0],
            came_up[0],
            came_down[0],
            came_up[1],
            came_down[2],
            came_up[2],
            came_down[1],
            from_back,
            from_front,
        ],
        axis=0,
    )
    return finish(own_t, received, recv_list, inv_mass, basis, fields)


def solution(mesh):
    placed = (
        P(("gx", "yz"), None),
        P(),
        P(),
        P(),
        P(("gx", "yz")),
        P(("gx", "yz")),
        P(("gx", "yz")),
        P(("gx", "yz")),
        P(("gx", "yz"), None),
        P(("gx", "yz"), None),
    )
    return jax.shard_map(
        on_device, mesh=mesh, in_specs=placed, out_specs=P(("gx", "yz"), None), check_vma=False
    )
```

```python
import functools

import jax
import jax.numpy as jnp
from jax import lax
from jax.experimental import pallas as pl
from jax.experimental.pallas import tpu as pltpu
from jax.sharding import PartitionSpec as P

F32 = jnp.float32
BF16 = jnp.bfloat16


def tet_kernel(
    zone_ref, table_ref, vol_ref, dest_ref, coeff_ref, bold_ref, bnew_ref, qw_ref,
    own_ref, up_ref, down_ref, ahead_ref, behind_ref, rise_ref, fall_ref, ct_ref, boldc_ref, bnewc_ref, qwt_ref, slot_ref, mom_ref, spread_ref,
    *, tables, basis, fields, zones, slots_pad
):
    step = pl.program_id(0)
    nt = (((1,), (1,)), ((), ()))
    width = basis * fields

    @pl.when(step == 0)
    def _():
        own_ref[...] = jnp.zeros_like(own_ref)
        slot_ref[...] = jnp.zeros_like(slot_ref)
        row = lax.broadcasted_iota(jnp.int32, (width, width), 0)
        col = lax.broadcasted_iota(jnp.int32, (width, width), 1)
        shuffle = (col == (row % basis) * fields + row // basis).astype(BF16)
        ct_ref[...] = lax.dot_general(shuffle, coeff_ref[...], nt, preferred_element_type=F32).astype(BF16)
        eye = (
            lax.broadcasted_iota(jnp.int32, (basis, basis), 0) == lax.broadcasted_iota(jnp.int32, (basis, basis), 1)
        ).astype(BF16)
        for t in range(tables):
            boldc_ref[:, t * basis : (t + 1) * basis] = bold_ref[t * basis : (t + 1) * basis, :]
            piece = bnew_ref[t * basis : (t + 1) * basis, :]
            bnewc_ref[:, t * basis : (t + 1) * basis] = lax.dot_general(
                eye, piece, nt, preferred_element_type=F32
            ).astype(BF16)
        weights = qw_ref[...]
        high = weights.astype(BF16)
        rest = weights - high.astype(F32)
        mid = rest.astype(BF16)
        low = (rest - mid.astype(F32)).astype(BF16)
        qwt_ref[...] = (
            lax.dot_general(eye, high, nt, preferred_element_type=F32)
            + lax.dot_general(eye, mid, nt, preferred_element_type=F32)
        ) + lax.dot_general(eye, low, nt, preferred_element_type=F32)

    block = zone_ref.shape[1]
    zone = zone_ref[...]
    zone_hot = (lax.broadcasted_iota(jnp.int32, (zones, block), 0) == zone).astype(BF16)
    picked = jnp.dot(ct_ref[...], zone_hot, preferred_element_type=F32).astype(BF16)
    table = table_ref[...]
    masks = [table == t for t in range(tables)]
    qwt = qwt_ref[...]
    scale = jnp.broadcast_to(qwt[:, 0:1], (basis, block))
    for t in range(1, tables):
        scale = jnp.where(masks[t], qwt[:, t : t + 1], scale)
    scale = scale * vol_ref[...]
    boldc = boldc_ref[...]
    bnewc = bnewc_ref[...]
    empty = jnp.zeros((basis, block), BF16)
    for f in range(fields):
        piece = picked[f * basis : (f + 1) * basis, :]
        for t in range(tables):
            spread_ref[t * basis : (t + 1) * basis, :] = jnp.where(masks[t], piece, empty)
        values = jnp.dot(boldc, spread_ref[...], preferred_element_type=F32)
        weighted = (scale * values).astype(BF16)
        for t in range(tables):
            spread_ref[t * basis : (t + 1) * basis, :] = jnp.where(masks[t], weighted, empty)
        mom_ref[f * basis : (f + 1) * basis, :] = jnp.dot(bnewc, spread_ref[...], preferred_element_type=F32)
    moments = mom_ref[...]
    high = moments.astype(BF16)
    low = (moments - high.astype(F32)).astype(BF16)
    dest = dest_ref[...]
    own_hot = (lax.broadcasted_iota(jnp.int32, (zones, block), 0) == dest).astype(BF16)
    own_ref[...] += lax.dot_general(high, own_hot, nt, preferred_element_type=F32) + lax.dot_general(
        low, own_hot, nt, preferred_element_type=F32
    )
    slot_hot = (lax.broadcasted_iota(jnp.int32, (slots_pad, block), 0) + zones == dest).astype(BF16)
    slot_ref[...] += lax.dot_general(slot_hot, high, nt, preferred_element_type=F32) + lax.dot_general(
        slot_hot, low, nt, preferred_element_type=F32
    )

    @pl.when(step == pl.num_programs(0) - 1)
    def _():
        cap = ahead_ref.shape[0]
        part = lambda k: slot_ref[k * cap : (k + 1) * cap, :].astype(BF16)
        for ref, ks in ((up_ref, (0, 4, 7)), (down_ref, (1, 5, 6))):
            for n, k in enumerate(ks):
                ref[n * cap : (n + 1) * cap, :] = part(k)
        ahead_ref[...] = part(8)
        behind_ref[...] = part(9)
        rise_ref[...] = part(2)
        fall_ref[...] = part(3)


def tet_partials(old_coeff, bold, bnew, quad_weight, zone, table, vol, dest, slots_pad, cap, block):
    tet_count = zone.shape[0]
    zones, width = old_coeff.shape
    tables = quad_weight.shape[0]
    basis = bold.shape[1]
    fields = width // basis
    kernel = functools.partial(
        tet_kernel, tables=tables, basis=basis, fields=fields, zones=zones, slots_pad=slots_pad
    )
    row_spec = pl.BlockSpec((1, block), lambda i: (0, i))
    whole = lambda shape: pl.BlockSpec(shape, lambda i: (0, 0))
    return pl.pallas_call(
        kernel,
        grid=(tet_count // block,),
        in_specs=[
            row_spec,
            row_spec,
            row_spec,
            row_spec,
            whole(old_coeff.shape),
            whole(bold.shape),
            whole(bnew.shape),
            whole(quad_weight.shape),
        ],
        out_specs=[whole((width, zones))] + [whole((3 * cap, width))] * 2 + [whole((cap, width))] * 4,
        out_shape=[jax.ShapeDtypeStruct((width, zones), F32)]
        + [jax.ShapeDtypeStruct((3 * cap, width), BF16)] * 2
        + [jax.ShapeDtypeStruct((cap, width), BF16)] * 4,
        scratch_shapes=[
            pltpu.VMEM((width, zones), BF16),
            pltpu.VMEM((basis, tables * basis), BF16),
            pltpu.VMEM((basis, tables * basis), BF16),
            pltpu.VMEM((basis, tables), F32),
            pltpu.VMEM((slots_pad, width), F32),
            pltpu.VMEM((width, block), F32),
            pltpu.VMEM((tables * basis, block), BF16),
        ],
        compiler_params=pltpu.CompilerParams(dimension_semantics=("arbitrary",)),
    )(
        zone.reshape(1, tet_count),
        table.reshape(1, tet_count),
        vol.reshape(1, tet_count),
        dest.reshape(1, tet_count),
        old_coeff,
        bold,
        bnew,
        quad_weight,
    )


def finish_kernel(
    own_ref, left_ref, right_ref, came_up_ref, came_down_ref, back_ref, front_ref, list_ref, inv_ref,
    out_ref, recv_ref, g_ref, h_ref, invt_ref, acc_ref, *, basis, fields
):
    width, zones = own_ref.shape
    slots = recv_ref.shape[0]
    cap = back_ref.shape[0]
    order = (
        (left_ref, 0), (right_ref, 0), (came_up_ref, 0), (came_down_ref, 0), (came_up_ref, 1),
        (came_down_ref, 2), (came_up_ref, 2), (came_down_ref, 1), (back_ref, 0), (front_ref, 0),
    )
    for k, (ref, n) in enumerate(order):
        recv_ref[k * cap : (k + 1) * cap, :] = ref[n * cap : (n + 1) * cap, :].astype(F32)
    slot_hot = (lax.broadcasted_iota(jnp.int32, (zones, slots), 0) == list_ref[...]).astype(F32)
    arrived = jnp.dot(slot_hot, recv_ref[...], preferred_element_type=F32)
    rounded = (own_ref[...] + arrived.T).astype(BF16).astype(F32)
    lanes = 128
    halves = zones // lanes
    for half in range(halves):
        g_ref[half * width : (half + 1) * width, :] = rounded[:, half * lanes : (half + 1) * lanes]
    for k in range(basis):
        for half in range(halves):
            h_ref[k * fields : (k + 1) * fields, half * lanes : (half + 1) * lanes] = g_ref[
                pl.ds(half * width + k, fields, stride=basis), :
            ]
    chunk = 128
    for c in range(basis * basis // chunk):
        invt_ref[c * chunk : (c + 1) * chunk, :] = inv_ref[:, c * chunk : (c + 1) * chunk].astype(F32).T

    chains = 8

    def body(j, carry):
        rows = invt_ref.at[pl.ds(pl.multiple_of(j * basis, basis), basis), :]
        sums = [jnp.zeros((fields, zones), F32) for _ in range(chains)]
        for k in range(basis):
            sums[k % chains] = sums[k % chains] + rows[k : k + 1, :] * h_ref[k * fields : (k + 1) * fields, :]
        while len(sums) > 1:
            sums = [sums[i] + sums[i + 1] for i in range(0, len(sums), 2)]
        acc_ref[pl.ds(pl.multiple_of(j * fields, fields), fields), :] = sums[0]
        return carry

    lax.fori_loop(0, basis, body, 0)
    out_ref[...] = acc_ref[...].T


def finish(own_t, received, recv_row, inv_mass, basis, fields):
    width, zones = own_t.shape
    kernel = functools.partial(finish_kernel, basis=basis, fields=fields)
    return pl.pallas_call(
        kernel,
        out_shape=jax.ShapeDtypeStruct((zones, width), F32),
        scratch_shapes=[
            pltpu.VMEM((recv_row.shape[1], width), F32),
            pltpu.VMEM((zones // 128 * width, 128), F32),
            pltpu.VMEM((width, zones), F32),
            pltpu.VMEM((basis * basis, zones), F32),
            pltpu.VMEM((width, zones), F32),
        ],
    )(own_t, *received, recv_row, inv_mass)


def shifted(block, axis, distance):
    count = lax.axis_size(axis)
    route = [(i, (i + distance) % count) for i in range(count)]
    return lax.ppermute(block, axis, route)


def on_device(
    old_coeff,
    basis_old,
    basis_new,
    quad_weight,
    tet_zone,
    tet_table,
    tet_volume,
    tet_dest,
    recv_list,
    inv_mass,
):
    zone_count, row_width = old_coeff.shape
    tables, quad, basis = basis_old.shape
    fields = row_width // basis
    slot_total = recv_list.shape[1]
    partner_count = 10
    slot_cap = slot_total // partner_count
    slots_pad = -(-slot_total // 128) * 128
    block = min(512, tet_zone.shape[0])

    bold = basis_old.reshape(tables * quad, basis)
    bnew = basis_new.reshape(tables * quad, basis)
    own_t, going_up, going_down, ahead, behind, rise, fall = tet_partials(
        old_coeff, bold, bnew, quad_weight, tet_zone, tet_table, tet_volume, tet_dest, slots_pad, slot_cap, block
    )
    lane_count = lax.axis_size("yz")
    face_side = 1 << (lane_count.bit_length() - 1) // 2
    from_left = shifted(going_up, "yz", 1)
    from_right = shifted(going_down, "yz", -1)
    from_back = shifted(ahead, "gx", 1)
    from_front = shifted(behind, "gx", -1)
    block_of = lambda x, n: x[n * slot_cap : (n + 1) * slot_cap]
    upward = jnp.concatenate([rise, block_of(from_left, 1), block_of(from_right, 2)], axis=0)
    downward = jnp.concatenate([fall, block_of(from_left, 2), block_of(from_right, 1)], axis=0)
    came_up = shifted(upward, "yz", face_side)
    came_down = shifted(downward, "yz", -face_side)
    received = (from_left, from_right, came_up, came_down, from_back, from_front)
    return finish(own_t, received, recv_list, inv_mass, basis, fields)


def solution(mesh):
    placed = (
        P(("gx", "yz"), None),
        P(),
        P(),
        P(),
        P(("gx", "yz")),
        P(("gx", "yz")),
        P(("gx", "yz")),
        P(("gx", "yz")),
        P(("gx", "yz"), None),
        P(("gx", "yz"), None),
    )
    return jax.shard_map(
        on_device, mesh=mesh, in_specs=placed, out_specs=P(("gx", "yz"), None), check_vma=False
    )
```

```python
import functools

import jax
import jax.numpy as jnp
from jax import lax
from jax.experimental import pallas as pl
from jax.experimental.pallas import tpu as pltpu
from jax.sharding import PartitionSpec as P

F32 = jnp.float32
BF16 = jnp.bfloat16


def tet_kernel(
    zone_ref, table_ref, vol_ref, dest_ref, coeff_ref, bold_ref, bnew_ref, qw_ref,
    own_ref, slot_out_ref, ct_ref, boldc_ref, bnewc_ref, qwt_ref, slot_ref, mom_ref, spread_ref,
    *, tables, basis, fields, zones, slots_pad
):
    step = pl.program_id(0)
    nt = (((1,), (1,)), ((), ()))
    width = basis * fields

    @pl.when(step == 0)
    def _():
        own_ref[...] = jnp.zeros_like(own_ref)
        slot_ref[...] = jnp.zeros_like(slot_ref)
        row = lax.broadcasted_iota(jnp.int32, (width, width), 0)
        col = lax.broadcasted_iota(jnp.int32, (width, width), 1)
        shuffle = (col == (row % basis) * fields + row // basis).astype(BF16)
        ct_ref[...] = lax.dot_general(shuffle, coeff_ref[...], nt, preferred_element_type=F32).astype(BF16)
        eye = (
            lax.broadcasted_iota(jnp.int32, (basis, basis), 0) == lax.broadcasted_iota(jnp.int32, (basis, basis), 1)
        ).astype(BF16)
        for t in range(tables):
            boldc_ref[:, t * basis : (t + 1) * basis] = bold_ref[t * basis : (t + 1) * basis, :]
            piece = bnew_ref[t * basis : (t + 1) * basis, :]
            bnewc_ref[:, t * basis : (t + 1) * basis] = lax.dot_general(
                eye, piece, nt, preferred_element_type=F32
            ).astype(BF16)
        weights = qw_ref[...]
        high = weights.astype(BF16)
        rest = weights - high.astype(F32)
        mid = rest.astype(BF16)
        low = (rest - mid.astype(F32)).astype(BF16)
        qwt_ref[...] = (
            lax.dot_general(eye, high, nt, preferred_element_type=F32)
            + lax.dot_general(eye, mid, nt, preferred_element_type=F32)
        ) + lax.dot_general(eye, low, nt, preferred_element_type=F32)

    block = zone_ref.shape[1]
    zone = zone_ref[...]
    zone_hot = (lax.broadcasted_iota(jnp.int32, (zones, block), 0) == zone).astype(BF16)
    picked = jnp.dot(ct_ref[...], zone_hot, preferred_element_type=F32).astype(BF16)
    table = table_ref[...]
    masks = [table == t for t in range(tables)]
    qwt = qwt_ref[...]
    scale = jnp.broadcast_to(qwt[:, 0:1], (basis, block))
    for t in range(1, tables):
        scale = jnp.where(masks[t], qwt[:, t : t + 1], scale)
    scale = scale * vol_ref[...]
    boldc = boldc_ref[...]
    bnewc = bnewc_ref[...]
    empty = jnp.zeros((basis, block), BF16)
    for f in range(fields):
        piece = picked[f * basis : (f + 1) * basis, :]
        for t in range(tables):
            spread_ref[t * basis : (t + 1) * basis, :] = jnp.where(masks[t], piece, empty)
        values = jnp.dot(boldc, spread_ref[...], preferred_element_type=F32)
        weighted = (scale * values).astype(BF16)
        for t in range(tables):
            spread_ref[t * basis : (t + 1) * basis, :] = jnp.where(masks[t], weighted, empty)
        mom_ref[f * basis : (f + 1) * basis, :] = jnp.dot(bnewc, spread_ref[...], preferred_element_type=F32)
    moments = mom_ref[...]
    high = moments.astype(BF16)
    low = (moments - high.astype(F32)).astype(BF16)
    dest = dest_ref[...]
    own_hot = (lax.broadcasted_iota(jnp.int32, (zones, block), 0) == dest).astype(BF16)
    own_ref[...] += lax.dot_general(high, own_hot, nt, preferred_element_type=F32) + lax.dot_general(
        low, own_hot, nt, preferred_element_type=F32
    )
    slot_hot = (lax.broadcasted_iota(jnp.int32, (slots_pad, block), 0) + zones == dest).astype(BF16)
    slot_ref[...] += lax.dot_general(slot_hot, high, nt, preferred_element_type=F32) + lax.dot_general(
        slot_hot, low, nt, preferred_element_type=F32
    )

    @pl.when(step == pl.num_programs(0) - 1)
    def _():
        slot_out_ref[...] = slot_ref[...].astype(BF16)


def tet_partials(old_coeff, bold, bnew, quad_weight, zone, table, vol, dest, slots_pad, block):
    tet_count = zone.shape[0]
    zones, width = old_coeff.shape
    tables = quad_weight.shape[0]
    basis = bold.shape[1]
    fields = width // basis
    kernel = functools.partial(
        tet_kernel, tables=tables, basis=basis, fields=fields, zones=zones, slots_pad=slots_pad
    )
    row_spec = pl.BlockSpec((1, block), lambda i: (0, i))
    whole = lambda shape: pl.BlockSpec(shape, lambda i: (0, 0))
    return pl.pallas_call(
        kernel,
        grid=(tet_count // block,),
        in_specs=[
            row_spec,
            row_spec,
            row_spec,
            row_spec,
            whole(old_coeff.shape),
            whole(bold.shape),
            whole(bnew.shape),
            whole(quad_weight.shape),
        ],
        out_specs=[whole((width, zones)), whole((slots_pad, width))],
        out_shape=[
            jax.ShapeDtypeStruct((width, zones), F32),
            jax.ShapeDtypeStruct((slots_pad, width), BF16),
        ],
        scratch_shapes=[
            pltpu.VMEM((width, zones), BF16),
            pltpu.VMEM((basis, tables * basis), BF16),
            pltpu.VMEM((basis, tables * basis), BF16),
            pltpu.VMEM((basis, tables), F32),
            pltpu.VMEM((slots_pad, width), F32),
            pltpu.VMEM((width, block), F32),
            pltpu.VMEM((tables * basis, block), BF16),
        ],
        compiler_params=pltpu.CompilerParams(dimension_semantics=("arbitrary",)),
    )(
        zone.reshape(1, tet_count),
        table.reshape(1, tet_count),
        vol.reshape(1, tet_count),
        dest.reshape(1, tet_count),
        old_coeff,
        bold,
        bnew,
        quad_weight,
    )


def finish_kernel(own_ref, recv_ref, list_ref, inv_ref, out_ref, g_ref, h_ref, invt_ref, acc_ref, *, basis, fields):
    width, zones = own_ref.shape
    slots = recv_ref.shape[0]
    slot_hot = (lax.broadcasted_iota(jnp.int32, (zones, slots), 0) == list_ref[...]).astype(F32)
    arrived = jnp.dot(slot_hot, recv_ref[...].astype(F32), preferred_element_type=F32)
    rounded = (own_ref[...] + arrived.T).astype(BF16).astype(F32)
    lanes = 128
    halves = zones // lanes
    for half in range(halves):
        g_ref[half * width : (half + 1) * width, :] = rounded[:, half * lanes : (half + 1) * lanes]
    for k in range(basis):
        for half in range(halves):
            h_ref[k * fields : (k + 1) * fields, half * lanes : (half + 1) * lanes] = g_ref[
                pl.ds(half * width + k, fields, stride=basis), :
            ]
    chunk = 128
    nt = (((1,), (1,)), ((), ()))
    eye = (
        lax.broadcasted_iota(jnp.int32, (chunk, chunk), 0) == lax.broadcasted_iota(jnp.int32, (chunk, chunk), 1)
    ).astype(BF16)
    for c in range(basis * basis // chunk):
        invt_ref[c * chunk : (c + 1) * chunk, :] = lax.dot_general(
            eye, inv_ref[:, c * chunk : (c + 1) * chunk], nt, preferred_element_type=F32
        )

    chains = 4
    pair = 2

    def body(jj, carry):
        rows = invt_ref.at[pl.ds(pl.multiple_of(jj * pair * basis, pair * basis), pair * basis), :]
        sums = [[jnp.zeros((fields, zones), F32) for _ in range(chains)] for _ in range(pair)]
        for k in range(basis):
            mass = h_ref[k * fields : (k + 1) * fields, :]
            for p in range(pair):
                sums[p][k % chains] = sums[p][k % chains] + rows[p * basis + k : p * basis + k + 1, :] * mass
        for p in range(pair):
            part = sums[p]
            while len(part) > 1:
                part = [part[i] + part[i + 1] for i in range(0, len(part), 2)]
            start = pl.multiple_of((jj * pair + p) * fields, fields)
            acc_ref[pl.ds(start, fields), :] = part[0]
        return carry

    lax.fori_loop(0, basis // pair, body, 0)
    out_ref[...] = acc_ref[...].T


def finish(own_t, received, recv_row, inv_mass, basis, fields):
    width, zones = own_t.shape
    kernel = functools.partial(finish_kernel, basis=basis, fields=fields)
    return pl.pallas_call(
        kernel,
        out_shape=jax.ShapeDtypeStruct((zones, width), F32),
        scratch_shapes=[
            pltpu.VMEM((zones // 128 * width, 128), F32),
            pltpu.VMEM((width, zones), F32),
            pltpu.VMEM((basis * basis, zones), F32),
            pltpu.VMEM((width, zones), F32),
        ],
    )(own_t, received, recv_row, inv_mass)


def shifted(block, axis, distance):
    count = lax.axis_size(axis)
    route = [(i, (i + distance) % count) for i in range(count)]
    return lax.ppermute(block, axis, route)


def on_device(
    old_coeff,
    basis_old,
    basis_new,
    quad_weight,
    tet_zone,
    tet_table,
    tet_volume,
    tet_dest,
    recv_list,
    inv_mass,
):
    zone_count, row_width = old_coeff.shape
    tables, quad, basis = basis_old.shape
    fields = row_width // basis
    slot_total = recv_list.shape[1]
    partner_count = 10
    slot_cap = slot_total // partner_count
    slots_pad = -(-slot_total // 128) * 128
    block = min(512, tet_zone.shape[0])

    bold = basis_old.reshape(tables * quad, basis)
    bnew = basis_new.reshape(tables * quad, basis)
    own_t, slot_rows = tet_partials(
        old_coeff, bold, bnew, quad_weight, tet_zone, tet_table, tet_volume, tet_dest, slots_pad, block
    )
    outgoing = slot_rows[:slot_total].reshape(partner_count, slot_cap, row_width)

    lane_count = lax.axis_size("yz")
    face_side = 1 << (lane_count.bit_length() - 1) // 2
    going_up = jnp.concatenate([outgoing[0], outgoing[4], outgoing[7]], axis=0)
    going_down = jnp.concatenate([outgoing[1], outgoing[5], outgoing[6]], axis=0)
    from_left = shifted(going_up, "yz", 1).reshape(3, slot_cap, row_width)
    from_right = shifted(going_down, "yz", -1).reshape(3, slot_cap, row_width)
    from_back = shifted(outgoing[8], "gx", 1)
    from_front = shifted(outgoing[9], "gx", -1)
    upward = jnp.concatenate([outgoing[2], from_left[1], from_right[2]], axis=0)
    downward = jnp.concatenate([outgoing[3], from_left[2], from_right[1]], axis=0)
    came_up = shifted(upward, "yz", face_side).reshape(3, slot_cap, row_width)
    came_down = shifted(downward, "yz", -face_side).reshape(3, slot_cap, row_width)
    received = jnp.concatenate(
        [
            from_left[0],
            from_right[0],
            came_up[0],
            came_down[0],
            came_up[1],
            came_down[2],
            came_up[2],
            came_down[1],
            from_back,
            from_front,
        ],
        axis=0,
    )
    return finish(own_t, received, recv_list, inv_mass, basis, fields)


def solution(mesh):
    placed = (
        P(("gx", "yz"), None),
        P(),
        P(),
        P(),
        P(("gx", "yz")),
        P(("gx", "yz")),
        P(("gx", "yz")),
        P(("gx", "yz")),
        P(("gx", "yz"), None),
        P(("gx", "yz"), None),
    )
    return jax.shard_map(
        on_device, mesh=mesh, in_specs=placed, out_specs=P(("gx", "yz"), None), check_vma=False
    )
```

```python
import functools

import jax
import jax.numpy as jnp
from jax import lax
from jax.experimental import pallas as pl
from jax.experimental.pallas import tpu as pltpu
from jax.sharding import PartitionSpec as P

F32 = jnp.float32
BF16 = jnp.bfloat16


def tet_kernel(
    zone_ref, table_ref, vol_ref, dest_ref, coeff_ref, bold_ref, bnew_ref, qw_ref,
    own_ref, slot_out_ref, ct_ref, boldc_ref, bnewc_ref, qwt_ref, slot_ref, mom_ref, spread_ref,
    *, tables, basis, fields, zones, slots_pad
):
    step = pl.program_id(0)
    nt = (((1,), (1,)), ((), ()))
    width = basis * fields

    @pl.when(step == 0)
    def _():
        own_ref[...] = jnp.zeros_like(own_ref)
        slot_ref[...] = jnp.zeros_like(slot_ref)
        row = lax.broadcasted_iota(jnp.int32, (width, width), 0)
        col = lax.broadcasted_iota(jnp.int32, (width, width), 1)
        shuffle = (col == (row % basis) * fields + row // basis).astype(BF16)
        ct_ref[...] = lax.dot_general(shuffle, coeff_ref[...], nt, preferred_element_type=F32).astype(BF16)
        eye = (
            lax.broadcasted_iota(jnp.int32, (basis, basis), 0) == lax.broadcasted_iota(jnp.int32, (basis, basis), 1)
        ).astype(BF16)
        for t in range(tables):
            boldc_ref[:, t * basis : (t + 1) * basis] = bold_ref[t * basis : (t + 1) * basis, :]
            piece = bnew_ref[t * basis : (t + 1) * basis, :]
            bnewc_ref[:, t * basis : (t + 1) * basis] = lax.dot_general(
                eye, piece, nt, preferred_element_type=F32
            ).astype(BF16)
        weights = qw_ref[...]
        high = weights.astype(BF16)
        rest = weights - high.astype(F32)
        mid = rest.astype(BF16)
        low = (rest - mid.astype(F32)).astype(BF16)
        qwt_ref[...] = (
            lax.dot_general(eye, high, nt, preferred_element_type=F32)
            + lax.dot_general(eye, mid, nt, preferred_element_type=F32)
        ) + lax.dot_general(eye, low, nt, preferred_element_type=F32)

    block = zone_ref.shape[1]
    zone = zone_ref[...]
    zone_hot = (lax.broadcasted_iota(jnp.int32, (zones, block), 0) == zone).astype(BF16)
    picked = jnp.dot(ct_ref[...], zone_hot, preferred_element_type=F32).astype(BF16)
    table = table_ref[...]
    masks = [table == t for t in range(tables)]
    qwt = qwt_ref[...]
    scale = jnp.broadcast_to(qwt[:, 0:1], (basis, block))
    for t in range(1, tables):
        scale = jnp.where(masks[t], qwt[:, t : t + 1], scale)
    scale = scale * vol_ref[...]
    boldc = boldc_ref[...]
    bnewc = bnewc_ref[...]
    empty = jnp.zeros((basis, block), BF16)
    for f in range(fields):
        piece = picked[f * basis : (f + 1) * basis, :]
        for t in range(tables):
            spread_ref[t * basis : (t + 1) * basis, :] = jnp.where(masks[t], piece, empty)
        values = jnp.dot(boldc, spread_ref[...], preferred_element_type=F32)
        weighted = (scale * values).astype(BF16)
        for t in range(tables):
            spread_ref[t * basis : (t + 1) * basis, :] = jnp.where(masks[t], weighted, empty)
        mom_ref[f * basis : (f + 1) * basis, :] = jnp.dot(bnewc, spread_ref[...], preferred_element_type=F32)
    moments = mom_ref[...]
    high = moments.astype(BF16)
    low = (moments - high.astype(F32)).astype(BF16)
    dest = dest_ref[...]
    own_hot = (lax.broadcasted_iota(jnp.int32, (zones, block), 0) == dest).astype(BF16)
    own_ref[...] += lax.dot_general(high, own_hot, nt, preferred_element_type=F32) + lax.dot_general(
        low, own_hot, nt, preferred_element_type=F32
    )
    slot_hot = (lax.broadcasted_iota(jnp.int32, (slots_pad, block), 0) + zones == dest).astype(BF16)
    slot_ref[...] += lax.dot_general(slot_hot, high, nt, preferred_element_type=F32) + lax.dot_general(
        slot_hot, low, nt, preferred_element_type=F32
    )

    @pl.when(step == pl.num_programs(0) - 1)
    def _():
        slot_out_ref[...] = slot_ref[...].astype(BF16)


def tet_partials(old_coeff, bold, bnew, quad_weight, zone, table, vol, dest, slots_pad, block):
    tet_count = zone.shape[0]
    zones, width = old_coeff.shape
    tables = quad_weight.shape[0]
    basis = bold.shape[1]
    fields = width // basis
    kernel = functools.partial(
        tet_kernel, tables=tables, basis=basis, fields=fields, zones=zones, slots_pad=slots_pad
    )
    row_spec = pl.BlockSpec((1, block), lambda i: (0, i))
    whole = lambda shape: pl.BlockSpec(shape, lambda i: (0, 0))
    return pl.pallas_call(
        kernel,
        grid=(tet_count // block,),
        in_specs=[
            row_spec,
            row_spec,
            row_spec,
            row_spec,
            whole(old_coeff.shape),
            whole(bold.shape),
            whole(bnew.shape),
            whole(quad_weight.shape),
        ],
        out_specs=[whole((width, zones)), whole((slots_pad, width))],
        out_shape=[
            jax.ShapeDtypeStruct((width, zones), F32),
            jax.ShapeDtypeStruct((slots_pad, width), BF16),
        ],
        scratch_shapes=[
            pltpu.VMEM((width, zones), BF16),
            pltpu.VMEM((basis, tables * basis), BF16),
            pltpu.VMEM((basis, tables * basis), BF16),
            pltpu.VMEM((basis, tables), F32),
            pltpu.VMEM((slots_pad, width), F32),
            pltpu.VMEM((width, block), F32),
            pltpu.VMEM((tables * basis, block), BF16),
        ],
        compiler_params=pltpu.CompilerParams(dimension_semantics=("arbitrary",)),
    )(
        zone.reshape(1, tet_count),
        table.reshape(1, tet_count),
        vol.reshape(1, tet_count),
        dest.reshape(1, tet_count),
        old_coeff,
        bold,
        bnew,
        quad_weight,
    )


def finish_kernel(own_ref, recv_ref, list_ref, inv_ref, out_ref, g_ref, h_ref, invt_ref, acc_ref, *, basis, fields):
    width, zones = own_ref.shape
    slots = recv_ref.shape[0]
    slot_hot = (lax.broadcasted_iota(jnp.int32, (zones, slots), 0) == list_ref[...]).astype(F32)
    arrived = jnp.dot(slot_hot, recv_ref[...].astype(F32), preferred_element_type=F32)
    rounded = (own_ref[...] + arrived.T).astype(BF16).astype(F32)
    lanes = 128
    halves = zones // lanes
    for half in range(halves):
        g_ref[half * width : (half + 1) * width, :] = rounded[:, half * lanes : (half + 1) * lanes]
    for k in range(basis):
        for half in range(halves):
            h_ref[k * fields : (k + 1) * fields, half * lanes : (half + 1) * lanes] = g_ref[
                pl.ds(half * width + k, fields, stride=basis), :
            ]
    chunk = 128
    nt = (((1,), (1,)), ((), ()))
    eye = (
        lax.broadcasted_iota(jnp.int32, (chunk, chunk), 0) == lax.broadcasted_iota(jnp.int32, (chunk, chunk), 1)
    ).astype(BF16)
    for c in range(basis * basis // chunk):
        invt_ref[c * chunk : (c + 1) * chunk, :] = lax.dot_general(
            eye, inv_ref[:, c * chunk : (c + 1) * chunk], nt, preferred_element_type=F32
        )

    chains = 4
    pair = 2

    def body(jj, carry):
        rows = invt_ref.at[pl.ds(pl.multiple_of(jj * pair * basis, pair * basis), pair * basis), :]
        sums = [[jnp.zeros((fields, zones), F32) for _ in range(chains)] for _ in range(pair)]
        for k in range(basis):
            mass = h_ref[k * fields : (k + 1) * fields, :]
            for p in range(pair):
                sums[p][k % chains] = sums[p][k % chains] + rows[p * basis + k : p * basis + k + 1, :] * mass
        for p in range(pair):
            part = sums[p]
            while len(part) > 1:
                part = [part[i] + part[i + 1] for i in range(0, len(part), 2)]
            start = pl.multiple_of((jj * pair + p) * fields, fields)
            acc_ref[pl.ds(start, fields), :] = part[0]
        return carry

    lax.fori_loop(0, basis // pair, body, 0)
    out_ref[...] = acc_ref[...].T


def finish(own_t, received, recv_row, inv_mass, basis, fields):
    width, zones = own_t.shape
    kernel = functools.partial(finish_kernel, basis=basis, fields=fields)
    return pl.pallas_call(
        kernel,
        out_shape=jax.ShapeDtypeStruct((zones, width), F32),
        scratch_shapes=[
            pltpu.VMEM((zones // 128 * width, 128), F32),
            pltpu.VMEM((width, zones), F32),
            pltpu.VMEM((basis * basis, zones), F32),
            pltpu.VMEM((width, zones), F32),
        ],
    )(own_t, received, recv_row, inv_mass)


def shifted(block, axis, distance):
    count = lax.axis_size(axis)
    route = [(i, (i + distance) % count) for i in range(count)]
    return lax.ppermute(block, axis, route)


def on_device(
    old_coeff,
    basis_old,
    basis_new,
    quad_weight,
    tet_zone,
    tet_table,
    tet_volume,
    tet_dest,
    recv_list,
    inv_mass,
):
    zone_count, row_width = old_coeff.shape
    tables, quad, basis = basis_old.shape
    fields = row_width // basis
    slot_total = recv_list.shape[1]
    partner_count = 10
    slot_cap = slot_total // partner_count
    slots_pad = -(-slot_total // 128) * 128
    block = min(2048, tet_zone.shape[0])

    bold = basis_old.reshape(tables * quad, basis)
    bnew = basis_new.reshape(tables * quad, basis)
    own_t, slot_rows = tet_partials(
        old_coeff, bold, bnew, quad_weight, tet_zone, tet_table, tet_volume, tet_dest, slots_pad, block
    )
    outgoing = slot_rows[:slot_total].reshape(partner_count, slot_cap, row_width)

    lane_count = lax.axis_size("yz")
    face_side = 1 << (lane_count.bit_length() - 1) // 2
    going_up = jnp.concatenate([outgoing[0], outgoing[4], outgoing[7]], axis=0)
    going_down = jnp.concatenate([outgoing[1], outgoing[5], outgoing[6]], axis=0)
    from_left = shifted(going_up, "yz", 1).reshape(3, slot_cap, row_width)
    from_right = shifted(going_down, "yz", -1).reshape(3, slot_cap, row_width)
    from_back = shifted(outgoing[8], "gx", 1)
    from_front = shifted(outgoing[9], "gx", -1)
    upward = jnp.concatenate([outgoing[2], from_left[1], from_right[2]], axis=0)
    downward = jnp.concatenate([outgoing[3], from_left[2], from_right[1]], axis=0)
    came_up = shifted(upward, "yz", face_side).reshape(3, slot_cap, row_width)
    came_down = shifted(downward, "yz", -face_side).reshape(3, slot_cap, row_width)
    received = jnp.concatenate(
        [
            from_left[0],
            from_right[0],
            came_up[0],
            came_down[0],
            came_up[1],
            came_down[2],
            came_up[2],
            came_down[1],
            from_back,
            from_front,
        ],
        axis=0,
    )
    return finish(own_t, received, recv_list, inv_mass, basis, fields)


def solution(mesh):
    placed = (
        P(("gx", "yz"), None),
        P(),
        P(),
        P(),
        P(("gx", "yz")),
        P(("gx", "yz")),
        P(("gx", "yz")),
        P(("gx", "yz")),
        P(("gx", "yz"), None),
        P(("gx", "yz"), None),
    )
    return jax.shard_map(
        on_device, mesh=mesh, in_specs=placed, out_specs=P(("gx", "yz"), None), check_vma=False
    )
```

```python
import functools

import jax
import jax.numpy as jnp
from jax import lax
from jax.experimental import pallas as pl
from jax.experimental.pallas import tpu as pltpu
from jax.sharding import PartitionSpec as P

F32 = jnp.float32
BF16 = jnp.bfloat16


def tet_kernel(
    zone_ref, table_ref, vol_ref, dest_ref, coeff_ref, bold_ref, bnew_ref, qw_ref,
    own_ref, slot_out_ref, ct_ref, boldc_ref, bnewc_ref, qwt_ref, slot_ref, mom_ref, spread_ref, mask_ref,
    *, tables, basis, fields, zones, slots_pad
):
    step = pl.program_id(0)
    nt = (((1,), (1,)), ((), ()))
    width = basis * fields

    @pl.when(step == 0)
    def _():
        own_ref[...] = jnp.zeros_like(own_ref)
        slot_ref[...] = jnp.zeros_like(slot_ref)
        row = lax.broadcasted_iota(jnp.int32, (width, width), 0)
        col = lax.broadcasted_iota(jnp.int32, (width, width), 1)
        shuffle = (col == (row % basis) * fields + row // basis).astype(BF16)
        ct_ref[...] = lax.dot_general(shuffle, coeff_ref[...], nt, preferred_element_type=F32).astype(BF16)
        eye = (
            lax.broadcasted_iota(jnp.int32, (basis, basis), 0) == lax.broadcasted_iota(jnp.int32, (basis, basis), 1)
        ).astype(BF16)
        for t in range(tables):
            boldc_ref[:, t * basis : (t + 1) * basis] = bold_ref[t * basis : (t + 1) * basis, :]
            piece = bnew_ref[t * basis : (t + 1) * basis, :]
            bnewc_ref[:, t * basis : (t + 1) * basis] = lax.dot_general(
                eye, piece, nt, preferred_element_type=F32
            ).astype(BF16)
        weights = qw_ref[...]
        high = weights.astype(BF16)
        rest = weights - high.astype(F32)
        mid = rest.astype(BF16)
        low = (rest - mid.astype(F32)).astype(BF16)
        qwt_ref[...] = (
            lax.dot_general(eye, high, nt, preferred_element_type=F32)
            + lax.dot_general(eye, mid, nt, preferred_element_type=F32)
        ) + lax.dot_general(eye, low, nt, preferred_element_type=F32)

    block = zone_ref.shape[1]
    zone = zone_ref[...]
    zone_hot = (lax.broadcasted_iota(jnp.int32, (zones, block), 0) == zone).astype(BF16)
    picked = jnp.dot(ct_ref[...], zone_hot, preferred_element_type=F32).astype(BF16)
    table = table_ref[...]
    masks = [table == t for t in range(tables)]
    qwt = qwt_ref[...]
    scale = jnp.broadcast_to(qwt[:, 0:1], (basis, block))
    for t in range(1, tables):
        scale = jnp.where(masks[t], qwt[:, t : t + 1], scale)
    scale = scale * vol_ref[...]
    boldc = boldc_ref[...]
    bnewc = bnewc_ref[...]
    for t in range(tables):
        mask_ref[t * basis : (t + 1) * basis, :] = jnp.broadcast_to(masks[t].astype(BF16), (basis, block))
    for f in range(fields):
        piece = picked[f * basis : (f + 1) * basis, :]
        for t in range(tables):
            spread_ref[t * basis : (t + 1) * basis, :] = piece * mask_ref[t * basis : (t + 1) * basis, :]
        values = jnp.dot(boldc, spread_ref[...], preferred_element_type=F32)
        weighted = (scale * values).astype(BF16)
        for t in range(tables):
            spread_ref[t * basis : (t + 1) * basis, :] = weighted * mask_ref[t * basis : (t + 1) * basis, :]
        mom_ref[f * basis : (f + 1) * basis, :] = jnp.dot(bnewc, spread_ref[...], preferred_element_type=F32)
    moments = mom_ref[...]
    high = moments.astype(BF16)
    low = (moments - high.astype(F32)).astype(BF16)
    dest = dest_ref[...]
    own_hot = (lax.broadcasted_iota(jnp.int32, (zones, block), 0) == dest).astype(BF16)
    own_ref[...] += lax.dot_general(high, own_hot, nt, preferred_element_type=F32) + lax.dot_general(
        low, own_hot, nt, preferred_element_type=F32
    )
    slot_hot = (lax.broadcasted_iota(jnp.int32, (slots_pad, block), 0) + zones == dest).astype(BF16)
    slot_ref[...] += lax.dot_general(slot_hot, high, nt, preferred_element_type=F32) + lax.dot_general(
        slot_hot, low, nt, preferred_element_type=F32
    )

    @pl.when(step == pl.num_programs(0) - 1)
    def _():
        slot_out_ref[...] = slot_ref[...].astype(BF16)


def tet_partials(old_coeff, bold, bnew, quad_weight, zone, table, vol, dest, slots_pad, block):
    tet_count = zone.shape[0]
    zones, width = old_coeff.shape
    tables = quad_weight.shape[0]
    basis = bold.shape[1]
    fields = width // basis
    kernel = functools.partial(
        tet_kernel, tables=tables, basis=basis, fields=fields, zones=zones, slots_pad=slots_pad
    )
    row_spec = pl.BlockSpec((1, block), lambda i: (0, i))
    whole = lambda shape: pl.BlockSpec(shape, lambda i: (0, 0))
    return pl.pallas_call(
        kernel,
        grid=(tet_count // block,),
        in_specs=[
            row_spec,
            row_spec,
            row_spec,
            row_spec,
            whole(old_coeff.shape),
            whole(bold.shape),
            whole(bnew.shape),
            whole(quad_weight.shape),
        ],
        out_specs=[whole((width, zones)), whole((slots_pad, width))],
        out_shape=[
            jax.ShapeDtypeStruct((width, zones), F32),
            jax.ShapeDtypeStruct((slots_pad, width), BF16),
        ],
        scratch_shapes=[
            pltpu.VMEM((width, zones), BF16),
            pltpu.VMEM((basis, tables * basis), BF16),
            pltpu.VMEM((basis, tables * basis), BF16),
            pltpu.VMEM((basis, tables), F32),
            pltpu.VMEM((slots_pad, width), F32),
            pltpu.VMEM((width, block), F32),
            pltpu.VMEM((tables * basis, block), BF16),
            pltpu.VMEM((tables * basis, block), BF16),
        ],
        compiler_params=pltpu.CompilerParams(dimension_semantics=("arbitrary",)),
    )(
        zone.reshape(1, tet_count),
        table.reshape(1, tet_count),
        vol.reshape(1, tet_count),
        dest.reshape(1, tet_count),
        old_coeff,
        bold,
        bnew,
        quad_weight,
    )


def finish_kernel(own_ref, recv_ref, list_ref, inv_ref, out_ref, g_ref, h_ref, invt_ref, acc_ref, *, basis, fields):
    width, zones = own_ref.shape
    slots = recv_ref.shape[0]
    slot_hot = (lax.broadcasted_iota(jnp.int32, (zones, slots), 0) == list_ref[...]).astype(F32)
    arrived = jnp.dot(slot_hot, recv_ref[...].astype(F32), preferred_element_type=F32)
    rounded = (own_ref[...] + arrived.T).astype(BF16).astype(F32)
    lanes = 128
    halves = zones // lanes
    for half in range(halves):
        g_ref[half * width : (half + 1) * width, :] = rounded[:, half * lanes : (half + 1) * lanes]
    for k in range(basis):
        for half in range(halves):
            h_ref[k * fields : (k + 1) * fields, half * lanes : (half + 1) * lanes] = g_ref[
                pl.ds(half * width + k, fields, stride=basis), :
            ]
    chunk = 128
    nt = (((1,), (1,)), ((), ()))
    eye = (
        lax.broadcasted_iota(jnp.int32, (chunk, chunk), 0) == lax.broadcasted_iota(jnp.int32, (chunk, chunk), 1)
    ).astype(BF16)
    for c in range(basis * basis // chunk):
        invt_ref[c * chunk : (c + 1) * chunk, :] = lax.dot_general(
            eye, inv_ref[:, c * chunk : (c + 1) * chunk], nt, preferred_element_type=F32
        )

    chains = 2
    pair = 4

    def body(jj, carry):
        rows = invt_ref.at[pl.ds(pl.multiple_of(jj * pair * basis, pair * basis), pair * basis), :]
        sums = [[jnp.zeros((fields, zones), F32) for _ in range(chains)] for _ in range(pair)]
        for k in range(basis):
            mass = h_ref[k * fields : (k + 1) * fields, :]
            for p in range(pair):
                sums[p][k % chains] = sums[p][k % chains] + rows[p * basis + k : p * basis + k + 1, :] * mass
        for p in range(pair):
            part = sums[p]
            while len(part) > 1:
                part = [part[i] + part[i + 1] for i in range(0, len(part), 2)]
            start = pl.multiple_of((jj * pair + p) * fields, fields)
            acc_ref[pl.ds(start, fields), :] = part[0]
        return carry

    lax.fori_loop(0, basis // pair, body, 0)
    out_ref[...] = acc_ref[...].T


def finish(own_t, received, recv_row, inv_mass, basis, fields):
    width, zones = own_t.shape
    kernel = functools.partial(finish_kernel, basis=basis, fields=fields)
    return pl.pallas_call(
        kernel,
        out_shape=jax.ShapeDtypeStruct((zones, width), F32),
        scratch_shapes=[
            pltpu.VMEM((zones // 128 * width, 128), F32),
            pltpu.VMEM((width, zones), F32),
            pltpu.VMEM((basis * basis, zones), F32),
            pltpu.VMEM((width, zones), F32),
        ],
    )(own_t, received, recv_row, inv_mass)


def shifted(block, axis, distance):
    count = lax.axis_size(axis)
    route = [(i, (i + distance) % count) for i in range(count)]
    return lax.ppermute(block, axis, route)


def on_device(
    old_coeff,
    basis_old,
    basis_new,
    quad_weight,
    tet_zone,
    tet_table,
    tet_volume,
    tet_dest,
    recv_list,
    inv_mass,
):
    zone_count, row_width = old_coeff.shape
    tables, quad, basis = basis_old.shape
    fields = row_width // basis
    slot_total = recv_list.shape[1]
    partner_count = 10
    slot_cap = slot_total // partner_count
    slots_pad = -(-slot_total // 128) * 128
    block = min(2048, tet_zone.shape[0])

    bold = basis_old.reshape(tables * quad, basis)
    bnew = basis_new.reshape(tables * quad, basis)
    own_t, slot_rows = tet_partials(
        old_coeff, bold, bnew, quad_weight, tet_zone, tet_table, tet_volume, tet_dest, slots_pad, block
    )
    outgoing = slot_rows[:slot_total].reshape(partner_count, slot_cap, row_width)

    lane_count = lax.axis_size("yz")
    face_side = 1 << (lane_count.bit_length() - 1) // 2
    going_up = jnp.concatenate([outgoing[0], outgoing[4], outgoing[7]], axis=0)
    going_down = jnp.concatenate([outgoing[1], outgoing[5], outgoing[6]], axis=0)
    from_left = shifted(going_up, "yz", 1).reshape(3, slot_cap, row_width)
    from_right = shifted(going_down, "yz", -1).reshape(3, slot_cap, row_width)
    from_back = shifted(outgoing[8], "gx", 1)
    from_front = shifted(outgoing[9], "gx", -1)
    upward = jnp.concatenate([outgoing[2], from_left[1], from_right[2]], axis=0)
    downward = jnp.concatenate([outgoing[3], from_left[2], from_right[1]], axis=0)
    came_up = shifted(upward, "yz", face_side).reshape(3, slot_cap, row_width)
    came_down = shifted(downward, "yz", -face_side).reshape(3, slot_cap, row_width)
    received = jnp.concatenate(
        [
            from_left[0],
            from_right[0],
            came_up[0],
            came_down[0],
            came_up[1],
            came_down[2],
            came_up[2],
            came_down[1],
            from_back,
            from_front,
        ],
        axis=0,
    )
    return finish(own_t, received, recv_list, inv_mass, basis, fields)


def solution(mesh):
    placed = (
        P(("gx", "yz"), None),
        P(),
        P(),
        P(),
        P(("gx", "yz")),
        P(("gx", "yz")),
        P(("gx", "yz")),
        P(("gx", "yz")),
        P(("gx", "yz"), None),
        P(("gx", "yz"), None),
    )
    return jax.shard_map(
        on_device, mesh=mesh, in_specs=placed, out_specs=P(("gx", "yz"), None), check_vma=False
    )
```

```python
import functools

import jax
import jax.numpy as jnp
from jax import lax
from jax.experimental import pallas as pl
from jax.experimental.pallas import tpu as pltpu
from jax.sharding import PartitionSpec as P

F32 = jnp.float32
BF16 = jnp.bfloat16


def tet_kernel(
    zone_ref, table_ref, vol_ref, dest_ref, coeff_ref, bold_ref, bnew_ref, qw_ref,
    own_ref, slot_out_ref, ct_ref, boldc_ref, bnewc_ref, qwt_ref, slot_ref, mom_ref, spread_ref,
    *, tables, basis, fields, zones, slots_pad
):
    step = pl.program_id(0)
    nt = (((1,), (1,)), ((), ()))
    width = basis * fields

    @pl.when(step == 0)
    def _():
        own_ref[...] = jnp.zeros_like(own_ref)
        slot_ref[...] = jnp.zeros_like(slot_ref)
        row = lax.broadcasted_iota(jnp.int32, (width, width), 0)
        col = lax.broadcasted_iota(jnp.int32, (width, width), 1)
        shuffle = (col == (row % basis) * fields + row // basis).astype(BF16)
        ct_ref[...] = lax.dot_general(shuffle, coeff_ref[...], nt, preferred_element_type=F32).astype(BF16)
        eye = (
            lax.broadcasted_iota(jnp.int32, (basis, basis), 0) == lax.broadcasted_iota(jnp.int32, (basis, basis), 1)
        ).astype(BF16)
        for t in range(tables):
            boldc_ref[:, t * basis : (t + 1) * basis] = bold_ref[t * basis : (t + 1) * basis, :]
            piece = bnew_ref[t * basis : (t + 1) * basis, :]
            bnewc_ref[:, t * basis : (t + 1) * basis] = lax.dot_general(
                eye, piece, nt, preferred_element_type=F32
            ).astype(BF16)
        weights = qw_ref[...]
        high = weights.astype(BF16)
        rest = weights - high.astype(F32)
        mid = rest.astype(BF16)
        low = (rest - mid.astype(F32)).astype(BF16)
        qwt_ref[...] = (
            lax.dot_general(eye, high, nt, preferred_element_type=F32)
            + lax.dot_general(eye, mid, nt, preferred_element_type=F32)
        ) + lax.dot_general(eye, low, nt, preferred_element_type=F32)

    block = zone_ref.shape[1]
    zone = zone_ref[...]
    zone_hot = (lax.broadcasted_iota(jnp.int32, (zones, block), 0) == zone).astype(BF16)
    picked = jnp.dot(ct_ref[...], zone_hot, preferred_element_type=F32).astype(BF16)
    table = table_ref[...]
    masks = [table == t for t in range(tables)]
    qwt = qwt_ref[...]
    scale = jnp.broadcast_to(qwt[:, 0:1], (basis, block))
    for t in range(1, tables):
        scale = jnp.where(masks[t], qwt[:, t : t + 1], scale)
    scale = scale * vol_ref[...]
    boldc = boldc_ref[...]
    bnewc = bnewc_ref[...]
    empty = jnp.zeros((basis, block), BF16)
    for f in range(fields):
        piece = picked[f * basis : (f + 1) * basis, :]
        for t in range(tables):
            spread_ref[t * basis : (t + 1) * basis, :] = jnp.where(masks[t], piece, empty)
        values = jnp.dot(boldc, spread_ref[...], preferred_element_type=F32)
        weighted = (scale * values).astype(BF16)
        for t in range(tables):
            spread_ref[t * basis : (t + 1) * basis, :] = jnp.where(masks[t], weighted, empty)
        mom_ref[f * basis : (f + 1) * basis, :] = jnp.dot(bnewc, spread_ref[...], preferred_element_type=F32)
    moments = mom_ref[...]
    high = moments.astype(BF16)
    low = (moments - high.astype(F32)).astype(BF16)
    dest = dest_ref[...]
    own_hot = (lax.broadcasted_iota(jnp.int32, (zones, block), 0) == dest).astype(BF16)
    own_ref[...] += lax.dot_general(high, own_hot, nt, preferred_element_type=F32) + lax.dot_general(
        low, own_hot, nt, preferred_element_type=F32
    )
    slot_hot = (lax.broadcasted_iota(jnp.int32, (slots_pad, block), 0) + zones == dest).astype(BF16)
    slot_ref[...] += lax.dot_general(slot_hot, high, nt, preferred_element_type=F32) + lax.dot_general(
        slot_hot, low, nt, preferred_element_type=F32
    )

    @pl.when(step == pl.num_programs(0) - 1)
    def _():
        slot_out_ref[...] = slot_ref[...].astype(BF16)


def tet_partials(old_coeff, bold, bnew, quad_weight, zone, table, vol, dest, slots_pad, block):
    tet_count = zone.shape[0]
    zones, width = old_coeff.shape
    tables = quad_weight.shape[0]
    basis = bold.shape[1]
    fields = width // basis
    kernel = functools.partial(
        tet_kernel, tables=tables, basis=basis, fields=fields, zones=zones, slots_pad=slots_pad
    )
    row_spec = pl.BlockSpec((1, block), lambda i: (0, i))
    whole = lambda shape: pl.BlockSpec(shape, lambda i: (0, 0))
    return pl.pallas_call(
        kernel,
        grid=(tet_count // block,),
        in_specs=[
            row_spec,
            row_spec,
            row_spec,
            row_spec,
            whole(old_coeff.shape),
            whole(bold.shape),
            whole(bnew.shape),
            whole(quad_weight.shape),
        ],
        out_specs=[whole((width, zones)), whole((slots_pad, width))],
        out_shape=[
            jax.ShapeDtypeStruct((width, zones), F32),
            jax.ShapeDtypeStruct((slots_pad, width), BF16),
        ],
        scratch_shapes=[
            pltpu.VMEM((width, zones), BF16),
            pltpu.VMEM((basis, tables * basis), BF16),
            pltpu.VMEM((basis, tables * basis), BF16),
            pltpu.VMEM((basis, tables), F32),
            pltpu.VMEM((slots_pad, width), F32),
            pltpu.VMEM((width, block), F32),
            pltpu.VMEM((tables * basis, block), BF16),
        ],
        compiler_params=pltpu.CompilerParams(dimension_semantics=("arbitrary",)),
    )(
        zone.reshape(1, tet_count),
        table.reshape(1, tet_count),
        vol.reshape(1, tet_count),
        dest.reshape(1, tet_count),
        old_coeff,
        bold,
        bnew,
        quad_weight,
    )


def finish_kernel(own_ref, recv_ref, list_ref, inv_ref, out_ref, g_ref, h_ref, invt_ref, acc_ref, *, basis, fields):
    width, zones = own_ref.shape
    slots = recv_ref.shape[0]
    slot_hot = (lax.broadcasted_iota(jnp.int32, (zones, slots), 0) == list_ref[...]).astype(F32)
    arrived = jnp.dot(slot_hot, recv_ref[...].astype(F32), preferred_element_type=F32)
    rounded = (own_ref[...] + arrived.T).astype(BF16).astype(F32)
    lanes = 128
    halves = zones // lanes
    for half in range(halves):
        g_ref[half * width : (half + 1) * width, :] = rounded[:, half * lanes : (half + 1) * lanes]
    for k in range(basis):
        for half in range(halves):
            h_ref[k * fields : (k + 1) * fields, half * lanes : (half + 1) * lanes] = g_ref[
                pl.ds(half * width + k, fields, stride=basis), :
            ]
    chunk = 128
    nt = (((1,), (1,)), ((), ()))
    eye = (
        lax.broadcasted_iota(jnp.int32, (chunk, chunk), 0) == lax.broadcasted_iota(jnp.int32, (chunk, chunk), 1)
    ).astype(BF16)
    for c in range(basis * basis // chunk):
        invt_ref[c * chunk : (c + 1) * chunk, :] = lax.dot_general(
            eye, inv_ref[:, c * chunk : (c + 1) * chunk], nt, preferred_element_type=F32
        )

    chains = 2
    pair = 4

    def body(jj, carry):
        rows = invt_ref.at[pl.ds(pl.multiple_of(jj * pair * basis, pair * basis), pair * basis), :]
        sums = [[jnp.zeros((fields, zones), F32) for _ in range(chains)] for _ in range(pair)]
        for k in range(basis):
            mass = h_ref[k * fields : (k + 1) * fields, :]
            for p in range(pair):
                sums[p][k % chains] = sums[p][k % chains] + rows[p * basis + k : p * basis + k + 1, :] * mass
        for p in range(pair):
            part = sums[p]
            while len(part) > 1:
                part = [part[i] + part[i + 1] for i in range(0, len(part), 2)]
            start = pl.multiple_of((jj * pair + p) * fields, fields)
            acc_ref[pl.ds(start, fields), :] = part[0]
        return carry

    lax.fori_loop(0, basis // pair, body, 0)
    out_ref[...] = acc_ref[...].T


def finish(own_t, received, recv_row, inv_mass, basis, fields):
    width, zones = own_t.shape
    kernel = functools.partial(finish_kernel, basis=basis, fields=fields)
    return pl.pallas_call(
        kernel,
        out_shape=jax.ShapeDtypeStruct((zones, width), F32),
        scratch_shapes=[
            pltpu.VMEM((zones // 128 * width, 128), F32),
            pltpu.VMEM((width, zones), F32),
            pltpu.VMEM((basis * basis, zones), F32),
            pltpu.VMEM((width, zones), F32),
        ],
    )(own_t, received, recv_row, inv_mass)


def shifted(block, axis, distance):
    count = lax.axis_size(axis)
    route = [(i, (i + distance) % count) for i in range(count)]
    return lax.ppermute(block, axis, route)


def on_device(
    old_coeff,
    basis_old,
    basis_new,
    quad_weight,
    tet_zone,
    tet_table,
    tet_volume,
    tet_dest,
    recv_list,
    inv_mass,
):
    zone_count, row_width = old_coeff.shape
    tables, quad, basis = basis_old.shape
    fields = row_width // basis
    slot_total = recv_list.shape[1]
    partner_count = 10
    slot_cap = slot_total // partner_count
    slots_pad = -(-slot_total // 128) * 128
    block = min(2048, tet_zone.shape[0])

    bold = basis_old.reshape(tables * quad, basis)
    bnew = basis_new.reshape(tables * quad, basis)
    own_t, slot_rows = tet_partials(
        old_coeff, bold, bnew, quad_weight, tet_zone, tet_table, tet_volume, tet_dest, slots_pad, block
    )
    outgoing = slot_rows[:slot_total].reshape(partner_count, slot_cap, row_width)

    lane_count = lax.axis_size("yz")
    face_side = 1 << (lane_count.bit_length() - 1) // 2
    going_up = jnp.concatenate([outgoing[0], outgoing[4], outgoing[7]], axis=0)
    going_down = jnp.concatenate([outgoing[1], outgoing[5], outgoing[6]], axis=0)
    from_left = shifted(going_up, "yz", 1).reshape(3, slot_cap, row_width)
    from_right = shifted(going_down, "yz", -1).reshape(3, slot_cap, row_width)
    from_back = shifted(outgoing[8], "gx", 1)
    from_front = shifted(outgoing[9], "gx", -1)
    upward = jnp.concatenate([outgoing[2], from_left[1], from_right[2]], axis=0)
    downward = jnp.concatenate([outgoing[3], from_left[2], from_right[1]], axis=0)
    came_up = shifted(upward, "yz", face_side).reshape(3, slot_cap, row_width)
    came_down = shifted(downward, "yz", -face_side).reshape(3, slot_cap, row_width)
    received = jnp.concatenate(
        [
            from_left[0],
            from_right[0],
            came_up[0],
            came_down[0],
            came_up[1],
            came_down[2],
            came_up[2],
            came_down[1],
            from_back,
            from_front,
        ],
        axis=0,
    )
    return finish(own_t, received, recv_list, inv_mass, basis, fields)


def solution(mesh):
    placed = (
        P(("gx", "yz"), None),
        P(),
        P(),
        P(),
        P(("gx", "yz")),
        P(("gx", "yz")),
        P(("gx", "yz")),
        P(("gx", "yz")),
        P(("gx", "yz"), None),
        P(("gx", "yz"), None),
    )
    return jax.shard_map(
        on_device, mesh=mesh, in_specs=placed, out_specs=P(("gx", "yz"), None), check_vma=False
    )
```

```python
import functools

import jax
import jax.numpy as jnp
from jax import lax
from jax.experimental import pallas as pl
from jax.experimental.pallas import tpu as pltpu
from jax.sharding import PartitionSpec as P

F32 = jnp.float32
BF16 = jnp.bfloat16


def tet_kernel(
    zone_ref, table_ref, vol_ref, dest_ref, coeff_ref, bold_ref, bnew_ref, qw_ref,
    own_ref, slot_out_ref, ct_ref, boldc_ref, bnewc_ref, qwt_ref, slot_ref, mom_ref, spread_ref, mask_ref,
    *, tables, basis, fields, zones, slots_pad
):
    step = pl.program_id(0)
    nt = (((1,), (1,)), ((), ()))
    width = basis * fields

    @pl.when(step == 0)
    def _():
        own_ref[...] = jnp.zeros_like(own_ref)
        slot_ref[...] = jnp.zeros_like(slot_ref)
        row = lax.broadcasted_iota(jnp.int32, (width, width), 0)
        col = lax.broadcasted_iota(jnp.int32, (width, width), 1)
        shuffle = (col == (row % basis) * fields + row // basis).astype(BF16)
        ct_ref[...] = lax.dot_general(shuffle, coeff_ref[...], nt, preferred_element_type=F32).astype(BF16)
        eye = (
            lax.broadcasted_iota(jnp.int32, (basis, basis), 0) == lax.broadcasted_iota(jnp.int32, (basis, basis), 1)
        ).astype(BF16)
        for t in range(tables):
            boldc_ref[:, t * basis : (t + 1) * basis] = bold_ref[t * basis : (t + 1) * basis, :]
            piece = bnew_ref[t * basis : (t + 1) * basis, :]
            bnewc_ref[:, t * basis : (t + 1) * basis] = lax.dot_general(
                eye, piece, nt, preferred_element_type=F32
            ).astype(BF16)
        weights = qw_ref[...]
        high = weights.astype(BF16)
        rest = weights - high.astype(F32)
        mid = rest.astype(BF16)
        low = (rest - mid.astype(F32)).astype(BF16)
        qwt_ref[...] = (
            lax.dot_general(eye, high, nt, preferred_element_type=F32)
            + lax.dot_general(eye, mid, nt, preferred_element_type=F32)
        ) + lax.dot_general(eye, low, nt, preferred_element_type=F32)

    block = zone_ref.shape[1]
    zone = zone_ref[...]
    zone_hot = (lax.broadcasted_iota(jnp.int32, (zones, block), 0) == zone).astype(BF16)
    picked = jnp.dot(ct_ref[...], zone_hot, preferred_element_type=F32).astype(BF16)
    table = table_ref[...]
    masks = [table == t for t in range(tables)]
    qwt = qwt_ref[...]
    scale = jnp.broadcast_to(qwt[:, 0:1], (basis, block))
    for t in range(1, tables):
        scale = jnp.where(masks[t], qwt[:, t : t + 1], scale)
    scale = scale * vol_ref[...]
    boldc = boldc_ref[...]
    bnewc = bnewc_ref[...]
    for t in range(tables):
        mask_ref[t * basis : (t + 1) * basis, :] = jnp.broadcast_to(masks[t].astype(BF16), (basis, block))
    for f in range(fields):
        piece = picked[f * basis : (f + 1) * basis, :]
        for t in range(tables):
            spread_ref[t * basis : (t + 1) * basis, :] = piece * mask_ref[t * basis : (t + 1) * basis, :]
        values = jnp.dot(boldc, spread_ref[...], preferred_element_type=F32)
        weighted = (scale * values).astype(BF16)
        for t in range(tables):
            spread_ref[t * basis : (t + 1) * basis, :] = weighted * mask_ref[t * basis : (t + 1) * basis, :]
        mom_ref[f * basis : (f + 1) * basis, :] = jnp.dot(bnewc, spread_ref[...], preferred_element_type=F32)
    moments = mom_ref[...]
    high = moments.astype(BF16)
    low = (moments - high.astype(F32)).astype(BF16)
    dest = dest_ref[...]
    own_hot = (lax.broadcasted_iota(jnp.int32, (zones, block), 0) == dest).astype(BF16)
    own_ref[...] += lax.dot_general(high, own_hot, nt, preferred_element_type=F32) + lax.dot_general(
        low, own_hot, nt, preferred_element_type=F32
    )
    slot_hot = (lax.broadcasted_iota(jnp.int32, (slots_pad, block), 0) + zones == dest).astype(BF16)
    slot_ref[...] += lax.dot_general(slot_hot, high, nt, preferred_element_type=F32) + lax.dot_general(
        slot_hot, low, nt, preferred_element_type=F32
    )

    @pl.when(step == pl.num_programs(0) - 1)
    def _():
        slot_out_ref[...] = slot_ref[...].astype(BF16)


def tet_partials(old_coeff, bold, bnew, quad_weight, zone, table, vol, dest, slots_pad, block):
    tet_count = zone.shape[0]
    zones, width = old_coeff.shape
    tables = quad_weight.shape[0]
    basis = bold.shape[1]
    fields = width // basis
    kernel = functools.partial(
        tet_kernel, tables=tables, basis=basis, fields=fields, zones=zones, slots_pad=slots_pad
    )
    row_spec = pl.BlockSpec((1, block), lambda i: (0, i))
    whole = lambda shape: pl.BlockSpec(shape, lambda i: (0, 0))
    return pl.pallas_call(
        kernel,
        grid=(tet_count // block,),
        in_specs=[
            row_spec,
            row_spec,
            row_spec,
            row_spec,
            whole(old_coeff.shape),
            whole(bold.shape),
            whole(bnew.shape),
            whole(quad_weight.shape),
        ],
        out_specs=[whole((width, zones)), whole((slots_pad, width))],
        out_shape=[
            jax.ShapeDtypeStruct((width, zones), F32),
            jax.ShapeDtypeStruct((slots_pad, width), BF16),
        ],
        scratch_shapes=[
            pltpu.VMEM((width, zones), BF16),
            pltpu.VMEM((basis, tables * basis), BF16),
            pltpu.VMEM((basis, tables * basis), BF16),
            pltpu.VMEM((basis, tables), F32),
            pltpu.VMEM((slots_pad, width), F32),
            pltpu.VMEM((width, block), F32),
            pltpu.VMEM((tables * basis, block), BF16),
            pltpu.VMEM((tables * basis, block), BF16),
        ],
        compiler_params=pltpu.CompilerParams(dimension_semantics=("arbitrary",)),
    )(
        zone.reshape(1, tet_count),
        table.reshape(1, tet_count),
        vol.reshape(1, tet_count),
        dest.reshape(1, tet_count),
        old_coeff,
        bold,
        bnew,
        quad_weight,
    )


def finish_kernel(own_ref, recv_ref, list_ref, inv_ref, out_ref, g_ref, h_ref, invt_ref, acc_ref, *, basis, fields):
    width, zones = own_ref.shape
    slots = recv_ref.shape[0]
    slot_hot = (lax.broadcasted_iota(jnp.int32, (zones, slots), 0) == list_ref[...]).astype(F32)
    arrived = jnp.dot(slot_hot, recv_ref[...].astype(F32), preferred_element_type=F32)
    rounded = (own_ref[...] + arrived.T).astype(BF16).astype(F32)
    lanes = 128
    halves = zones // lanes
    for half in range(halves):
        g_ref[half * width : (half + 1) * width, :] = rounded[:, half * lanes : (half + 1) * lanes]
    for k in range(basis):
        for half in range(halves):
            h_ref[k * fields : (k + 1) * fields, half * lanes : (half + 1) * lanes] = g_ref[
                pl.ds(half * width + k, fields, stride=basis), :
            ]
    chunk = 128
    nt = (((1,), (1,)), ((), ()))
    eye = (
        lax.broadcasted_iota(jnp.int32, (chunk, chunk), 0) == lax.broadcasted_iota(jnp.int32, (chunk, chunk), 1)
    ).astype(BF16)
    for c in range(basis * basis // chunk):
        invt_ref[c * chunk : (c + 1) * chunk, :] = lax.dot_general(
            eye, inv_ref[:, c * chunk : (c + 1) * chunk], nt, preferred_element_type=F32
        )

    chains = 2
    pair = 4

    def body(jj, carry):
        rows = invt_ref.at[pl.ds(pl.multiple_of(jj * pair * basis, pair * basis), pair * basis), :]
        sums = [[jnp.zeros((fields, zones), F32) for _ in range(chains)] for _ in range(pair)]
        for k in range(basis):
            mass = h_ref[k * fields : (k + 1) * fields, :]
            for p in range(pair):
                sums[p][k % chains] = sums[p][k % chains] + rows[p * basis + k : p * basis + k + 1, :] * mass
        for p in range(pair):
            part = sums[p]
            while len(part) > 1:
                part = [part[i] + part[i + 1] for i in range(0, len(part), 2)]
            start = pl.multiple_of((jj * pair + p) * fields, fields)
            acc_ref[pl.ds(start, fields), :] = part[0]
        return carry

    lax.fori_loop(0, basis // pair, body, 0)
    out_ref[...] = acc_ref[...].T


def finish(own_t, received, recv_row, inv_mass, basis, fields):
    width, zones = own_t.shape
    kernel = functools.partial(finish_kernel, basis=basis, fields=fields)
    return pl.pallas_call(
        kernel,
        out_shape=jax.ShapeDtypeStruct((zones, width), F32),
        scratch_shapes=[
            pltpu.VMEM((zones // 128 * width, 128), F32),
            pltpu.VMEM((width, zones), F32),
            pltpu.VMEM((basis * basis, zones), F32),
            pltpu.VMEM((width, zones), F32),
        ],
    )(own_t, received, recv_row, inv_mass)


def split_shift(up_block, down_block, axis, distance, far_up, far_down):
    count = lax.axis_size(axis)
    up_near = [(i, (i + distance) % count) for i in range(count) if not far_up(i)]
    down_near = [(i, (i - distance) % count) for i in range(count) if not far_down(i)]
    far = [(i, (i + distance) % count) for i in range(count) if far_up(i)]
    far += [(i, (i - distance) % count) for i in range(count) if far_down(i)]
    here = lax.axis_index(axis)
    near_left = lax.ppermute(up_block, axis, up_near)
    near_right = lax.ppermute(down_block, axis, down_near)
    wrapped = lax.ppermute(jnp.where(far_up(here), up_block, down_block), axis, far)
    from_left = jnp.where(far_up((here - distance) % count), wrapped, near_left)
    from_right = jnp.where(far_down((here + distance) % count), wrapped, near_right)
    return from_left, from_right


def shifted(block, axis, distance):
    count = lax.axis_size(axis)
    route = [(i, (i + distance) % count) for i in range(count)]
    return lax.ppermute(block, axis, route)


def on_device(
    old_coeff,
    basis_old,
    basis_new,
    quad_weight,
    tet_zone,
    tet_table,
    tet_volume,
    tet_dest,
    recv_list,
    inv_mass,
):
    zone_count, row_width = old_coeff.shape
    tables, quad, basis = basis_old.shape
    fields = row_width // basis
    slot_total = recv_list.shape[1]
    partner_count = 10
    slot_cap = slot_total // partner_count
    slots_pad = -(-slot_total // 128) * 128
    block = min(2048, tet_zone.shape[0])

    bold = basis_old.reshape(tables * quad, basis)
    bnew = basis_new.reshape(tables * quad, basis)
    own_t, slot_rows = tet_partials(
        old_coeff, bold, bnew, quad_weight, tet_zone, tet_table, tet_volume, tet_dest, slots_pad, block
    )
    outgoing = slot_rows[:slot_total].reshape(partner_count, slot_cap, row_width)

    lane_count = lax.axis_size("yz")
    face_side = 1 << (lane_count.bit_length() - 1) // 2
    going_up = jnp.concatenate([outgoing[0], outgoing[4], outgoing[7]], axis=0)
    going_down = jnp.concatenate([outgoing[1], outgoing[5], outgoing[6]], axis=0)
    from_left, from_right = split_shift(
        going_up, going_down, "yz", 1, lambda i: i % face_side == face_side - 1, lambda i: i % face_side == 0
    )
    from_left = from_left.reshape(3, slot_cap, row_width)
    from_right = from_right.reshape(3, slot_cap, row_width)
    from_back = shifted(outgoing[8], "gx", 1)
    from_front = shifted(outgoing[9], "gx", -1)
    upward = jnp.concatenate([outgoing[2], from_left[1], from_right[2]], axis=0)
    downward = jnp.concatenate([outgoing[3], from_left[2], from_right[1]], axis=0)
    came_up, came_down = split_shift(
        upward, downward, "yz", face_side, lambda i: i >= lane_count - face_side, lambda i: i < face_side
    )
    came_up = came_up.reshape(3, slot_cap, row_width)
    came_down = came_down.reshape(3, slot_cap, row_width)
    received = jnp.concatenate(
        [
            from_left[0],
            from_right[0],
            came_up[0],
            came_down[0],
            came_up[1],
            came_down[2],
            came_up[2],
            came_down[1],
            from_back,
            from_front,
        ],
        axis=0,
    )
    return finish(own_t, received, recv_list, inv_mass, basis, fields)


def solution(mesh):
    placed = (
        P(("gx", "yz"), None),
        P(),
        P(),
        P(),
        P(("gx", "yz")),
        P(("gx", "yz")),
        P(("gx", "yz")),
        P(("gx", "yz")),
        P(("gx", "yz"), None),
        P(("gx", "yz"), None),
    )
    return jax.shard_map(
        on_device, mesh=mesh, in_specs=placed, out_specs=P(("gx", "yz"), None), check_vma=False
    )
```

```python
import functools

import jax
import jax.numpy as jnp
from jax import lax
from jax.experimental import pallas as pl
from jax.experimental.pallas import tpu as pltpu
from jax.sharding import PartitionSpec as P

F32 = jnp.float32
BF16 = jnp.bfloat16


def tet_kernel(
    zone_ref, table_ref, vol_ref, dest_ref, coeff_ref, bold_ref, bnew_ref, qw_ref,
    own_ref, slot_out_ref, ct_ref, boldc_ref, bnewc_ref, qwt_ref, slot_ref, mom_ref, spread_ref, mask_ref,
    *, tables, basis, fields, zones, slots_pad, single
):
    step = pl.program_id(0)
    nt = (((1,), (1,)), ((), ()))
    width = basis * fields

    @pl.when(step == 0)
    def _():
        if not single:
            own_ref[...] = jnp.zeros_like(own_ref)
            slot_ref[...] = jnp.zeros_like(slot_ref)
        row = lax.broadcasted_iota(jnp.int32, (width, width), 0)
        col = lax.broadcasted_iota(jnp.int32, (width, width), 1)
        shuffle = (col == (row % basis) * fields + row // basis).astype(BF16)
        ct_ref[...] = lax.dot_general(shuffle, coeff_ref[...], nt, preferred_element_type=F32).astype(BF16)
        eye = (
            lax.broadcasted_iota(jnp.int32, (basis, basis), 0) == lax.broadcasted_iota(jnp.int32, (basis, basis), 1)
        ).astype(BF16)
        for t in range(tables):
            boldc_ref[:, t * basis : (t + 1) * basis] = bold_ref[t * basis : (t + 1) * basis, :]
            piece = bnew_ref[t * basis : (t + 1) * basis, :]
            bnewc_ref[:, t * basis : (t + 1) * basis] = lax.dot_general(
                eye, piece, nt, preferred_element_type=F32
            ).astype(BF16)
        weights = qw_ref[...]
        high = weights.astype(BF16)
        rest = weights - high.astype(F32)
        mid = rest.astype(BF16)
        low = (rest - mid.astype(F32)).astype(BF16)
        qwt_ref[...] = (
            lax.dot_general(eye, high, nt, preferred_element_type=F32)
            + lax.dot_general(eye, mid, nt, preferred_element_type=F32)
        ) + lax.dot_general(eye, low, nt, preferred_element_type=F32)

    block = zone_ref.shape[1]
    zone = zone_ref[...]
    zone_hot = (lax.broadcasted_iota(jnp.int32, (zones, block), 0) == zone).astype(BF16)
    picked = jnp.dot(ct_ref[...], zone_hot, preferred_element_type=F32).astype(BF16)
    table = table_ref[...]
    masks = [table == t for t in range(tables)]
    qwt = qwt_ref[...]
    scale = jnp.broadcast_to(qwt[:, 0:1], (basis, block))
    for t in range(1, tables):
        scale = jnp.where(masks[t], qwt[:, t : t + 1], scale)
    scale = scale * vol_ref[...]
    boldc = boldc_ref[...]
    bnewc = bnewc_ref[...]
    for t in range(tables):
        mask_ref[t * basis : (t + 1) * basis, :] = jnp.broadcast_to(masks[t].astype(BF16), (basis, block))
    for f in range(fields):
        piece = picked[f * basis : (f + 1) * basis, :]
        for t in range(tables):
            spread_ref[t * basis : (t + 1) * basis, :] = piece * mask_ref[t * basis : (t + 1) * basis, :]
        values = jnp.dot(boldc, spread_ref[...], preferred_element_type=F32)
        weighted = (scale * values).astype(BF16)
        for t in range(tables):
            spread_ref[t * basis : (t + 1) * basis, :] = weighted * mask_ref[t * basis : (t + 1) * basis, :]
        mom_ref[f * basis : (f + 1) * basis, :] = jnp.dot(bnewc, spread_ref[...], preferred_element_type=F32)
    moments = mom_ref[...]
    high = moments.astype(BF16)
    low = (moments - high.astype(F32)).astype(BF16)
    dest = dest_ref[...]
    own_hot = (lax.broadcasted_iota(jnp.int32, (zones, block), 0) == dest).astype(BF16)
    own_part = lax.dot_general(high, own_hot, nt, preferred_element_type=F32) + lax.dot_general(
        low, own_hot, nt, preferred_element_type=F32
    )
    slot_hot = (lax.broadcasted_iota(jnp.int32, (slots_pad, block), 0) + zones == dest).astype(BF16)
    slot_part = lax.dot_general(slot_hot, high, nt, preferred_element_type=F32) + lax.dot_general(
        slot_hot, low, nt, preferred_element_type=F32
    )
    if single:
        own_ref[...] = own_part
        slot_out_ref[...] = slot_part.astype(BF16)
    else:
        own_ref[...] += own_part
        slot_ref[...] += slot_part

        @pl.when(step == pl.num_programs(0) - 1)
        def _():
            slot_out_ref[...] = slot_ref[...].astype(BF16)


def tet_partials(old_coeff, bold, bnew, quad_weight, zone, table, vol, dest, slots_pad, block):
    tet_count = zone.shape[0]
    zones, width = old_coeff.shape
    tables = quad_weight.shape[0]
    basis = bold.shape[1]
    fields = width // basis
    kernel = functools.partial(
        tet_kernel, tables=tables, basis=basis, fields=fields, zones=zones, slots_pad=slots_pad,
        single=tet_count == block,
    )
    row_spec = pl.BlockSpec((1, block), lambda i: (0, i))
    whole = lambda shape: pl.BlockSpec(shape, lambda i: (0, 0))
    return pl.pallas_call(
        kernel,
        grid=(tet_count // block,),
        in_specs=[
            row_spec,
            row_spec,
            row_spec,
            row_spec,
            whole(old_coeff.shape),
            whole(bold.shape),
            whole(bnew.shape),
            whole(quad_weight.shape),
        ],
        out_specs=[whole((width, zones)), whole((slots_pad, width))],
        out_shape=[
            jax.ShapeDtypeStruct((width, zones), F32),
            jax.ShapeDtypeStruct((slots_pad, width), BF16),
        ],
        scratch_shapes=[
            pltpu.VMEM((width, zones), BF16),
            pltpu.VMEM((basis, tables * basis), BF16),
            pltpu.VMEM((basis, tables * basis), BF16),
            pltpu.VMEM((basis, tables), F32),
            pltpu.VMEM((slots_pad, width), F32),
            pltpu.VMEM((width, block), F32),
            pltpu.VMEM((tables * basis, block), BF16),
            pltpu.VMEM((tables * basis, block), BF16),
        ],
        compiler_params=pltpu.CompilerParams(dimension_semantics=("arbitrary",)),
    )(
        zone.reshape(1, tet_count),
        table.reshape(1, tet_count),
        vol.reshape(1, tet_count),
        dest.reshape(1, tet_count),
        old_coeff,
        bold,
        bnew,
        quad_weight,
    )


def finish_kernel(own_ref, recv_ref, list_ref, inv_ref, out_ref, g_ref, h_ref, invt_ref, acc_ref, *, basis, fields):
    width, zones = own_ref.shape
    slots = recv_ref.shape[0]
    slot_hot = (lax.broadcasted_iota(jnp.int32, (zones, slots), 0) == list_ref[...]).astype(F32)
    arrived = jnp.dot(slot_hot, recv_ref[...].astype(F32), preferred_element_type=F32)
    rounded = (own_ref[...] + arrived.T).astype(BF16).astype(F32)
    lanes = 128
    halves = zones // lanes
    for half in range(halves):
        g_ref[half * width : (half + 1) * width, :] = rounded[:, half * lanes : (half + 1) * lanes]
    for k in range(basis):
        for half in range(halves):
            h_ref[k * fields : (k + 1) * fields, half * lanes : (half + 1) * lanes] = g_ref[
                pl.ds(half * width + k, fields, stride=basis), :
            ]
    chunk = 128
    nt = (((1,), (1,)), ((), ()))
    eye = (
        lax.broadcasted_iota(jnp.int32, (chunk, chunk), 0) == lax.broadcasted_iota(jnp.int32, (chunk, chunk), 1)
    ).astype(BF16)
    for c in range(basis * basis // chunk):
        invt_ref[c * chunk : (c + 1) * chunk, :] = lax.dot_general(
            eye, inv_ref[:, c * chunk : (c + 1) * chunk], nt, preferred_element_type=F32
        )

    chains = 2
    pair = 4

    def body(jj, carry):
        rows = invt_ref.at[pl.ds(pl.multiple_of(jj * pair * basis, pair * basis), pair * basis), :]
        sums = [[jnp.zeros((fields, zones), F32) for _ in range(chains)] for _ in range(pair)]
        for k in range(basis):
            mass = h_ref[k * fields : (k + 1) * fields, :]
            for p in range(pair):
                sums[p][k % chains] = sums[p][k % chains] + rows[p * basis + k : p * basis + k + 1, :] * mass
        for p in range(pair):
            part = sums[p]
            while len(part) > 1:
                part = [part[i] + part[i + 1] for i in range(0, len(part), 2)]
            start = pl.multiple_of((jj * pair + p) * fields, fields)
            acc_ref[pl.ds(start, fields), :] = part[0]
        return carry

    lax.fori_loop(0, basis // pair, body, 0)
    out_ref[...] = acc_ref[...].T


def finish(own_t, received, recv_row, inv_mass, basis, fields):
    width, zones = own_t.shape
    kernel = functools.partial(finish_kernel, basis=basis, fields=fields)
    return pl.pallas_call(
        kernel,
        out_shape=jax.ShapeDtypeStruct((zones, width), F32),
        scratch_shapes=[
            pltpu.VMEM((zones // 128 * width, 128), F32),
            pltpu.VMEM((width, zones), F32),
            pltpu.VMEM((basis * basis, zones), F32),
            pltpu.VMEM((width, zones), F32),
        ],
    )(own_t, received, recv_row, inv_mass)


def shifted(block, axis, distance):
    count = lax.axis_size(axis)
    route = [(i, (i + distance) % count) for i in range(count)]
    return lax.ppermute(block, axis, route)


def on_device(
    old_coeff,
    basis_old,
    basis_new,
    quad_weight,
    tet_zone,
    tet_table,
    tet_volume,
    tet_dest,
    recv_list,
    inv_mass,
):
    zone_count, row_width = old_coeff.shape
    tables, quad, basis = basis_old.shape
    fields = row_width // basis
    slot_total = recv_list.shape[1]
    partner_count = 10
    slot_cap = slot_total // partner_count
    slots_pad = -(-slot_total // 128) * 128
    block = min(2048, tet_zone.shape[0])

    bold = basis_old.reshape(tables * quad, basis)
    bnew = basis_new.reshape(tables * quad, basis)
    own_t, slot_rows = tet_partials(
        old_coeff, bold, bnew, quad_weight, tet_zone, tet_table, tet_volume, tet_dest, slots_pad, block
    )
    outgoing = slot_rows[:slot_total].reshape(partner_count, slot_cap, row_width)

    lane_count = lax.axis_size("yz")
    face_side = 1 << (lane_count.bit_length() - 1) // 2
    going_up = jnp.concatenate([outgoing[0], outgoing[4], outgoing[7]], axis=0)
    going_down = jnp.concatenate([outgoing[1], outgoing[5], outgoing[6]], axis=0)
    from_left = shifted(going_up, "yz", 1).reshape(3, slot_cap, row_width)
    from_right = shifted(going_down, "yz", -1).reshape(3, slot_cap, row_width)
    from_back = shifted(outgoing[8], "gx", 1)
    from_front = shifted(outgoing[9], "gx", -1)
    upward = jnp.concatenate([outgoing[2], from_left[1], from_right[2]], axis=0)
    downward = jnp.concatenate([outgoing[3], from_left[2], from_right[1]], axis=0)
    came_up = shifted(upward, "yz", face_side).reshape(3, slot_cap, row_width)
    came_down = shifted(downward, "yz", -face_side).reshape(3, slot_cap, row_width)
    received = jnp.concatenate(
        [
            from_left[0],
            from_right[0],
            came_up[0],
            came_down[0],
            came_up[1],
            came_down[2],
            came_up[2],
            came_down[1],
            from_back,
            from_front,
        ],
        axis=0,
    )
    return finish(own_t, received, recv_list, inv_mass, basis, fields)


def solution(mesh):
    placed = (
        P(("gx", "yz"), None),
        P(),
        P(),
        P(),
        P(("gx", "yz")),
        P(("gx", "yz")),
        P(("gx", "yz")),
        P(("gx", "yz")),
        P(("gx", "yz"), None),
        P(("gx", "yz"), None),
    )
    return jax.shard_map(
        on_device, mesh=mesh, in_specs=placed, out_specs=P(("gx", "yz"), None), check_vma=False
    )
```
